256 devices in a mesh: dp: 4 (over x_lo, core), expert: 64 (over z, y, x_hi).
Axes of the slice: x: 4 (x_hi: 2, x_lo: 2; x = x_hi * 2 + x_lo), y: 4, z: 8, core: 2. Of those that a mesh axis runs over, the one named last changes fastest.
Arguments:
- prev_acts: bfloat16 [4, 64, 128, 3584], P('dp', 'expert'), may hold values from -6 to 6
- prev_cot: bfloat16 [4, 64, 128, 512], P('dp', 'expert'), may hold values from -0.59765625 to 0.59765625
- weights: bfloat16 [64, 3584, 512], P('expert', 'dp'), may hold values from -0.09375 to 0.09375
- first_moment: float32 [64, 3584, 512], P('expert', 'dp'), may hold values from -1.8 to 1.8
- second_moment: float32 [64, 3584, 512], P('expert', 'dp'), may hold values from 0.1 to 2
- tokens: bfloat16 [4, 64, 128, 3584], P('dp', 'expert'), may hold values from -6 to 6
- routing: int32 [4, 64, 128, 2], P('dp', 'expert'), may hold values from 0 to 15, all different within a row; in each aligned block of 128 rows (0 to 127, 128 to 255, ..., all dimensions but the last counted through in order) at most 24 rows name the same one
- gates: bfloat16 [4, 64, 128, 2], P('dp', 'expert'), may hold values from 0.19921875 to 1
- token_counts: int32 [4, 64], P('dp', 'expert'), may hold values from 64 to 128
- old_owner: int32 [16], replicated, may hold values from 0 to 15, each once
- new_owner: int32 [16], replicated, may hold values from 0 to 15, each once
Outputs:
- expert_hidden: bfloat16 [4, 64, 1536, 256], P('dp', 'expert')
- new_weights: bfloat16 [64, 3584, 512], P('expert', 'dp')
- new_first: float32 [64, 3584, 512], P('expert', 'dp')
- new_second: float32 [64, 3584, 512], P('expert', 'dp')
The draws below stay inside these ranges and needn't reach their ends.
Inputs may be any that keep to these rules, and one draw needn't show every extreme that they name: `routing`: each token names 2 different hot experts; within the rows of one device no hot expert is named by more than 24 rows. `old_owner`: each is a permutation of the 16 groups. `new_owner`: each is a permutation of the 16 groups.
All inputs are finite; a program needn't handle non-finite values.
Results may differ from the reference program's by a relative error of at most 0.013.
Values may be sent and summed in bfloat16 or wider, within the bound.
No kernel may reach another device: no remote copies, remote signals or barrier semaphores. Data moves between devices by JAX's collectives and lax.ppermute only.
A program may use at most 128 MiB of HBM per device.

```python
import math
import jax
import jax.numpy as jnp
import numpy as np
from jax import lax

D = 3584
GRP = 4
TOPH = 2
TOK_DEV = 128
GRAD_ROWS = 128
HID = 256
HOT = 16
CAP = 24
N_DP = 4
N_EXPERT = 64


def draw_token_counts(key, part):
    count_key = jax.random.fold_in(key, 11)
    chosen_key = jax.random.fold_in(key, 12)
    counts = jax.random.randint(count_key, (N_DP * N_EXPERT,), TOK_DEV // 2, TOK_DEV + 1, dtype=jnp.int32)
    chosen = jax.random.randint(chosen_key, (), 0, N_DP * N_EXPERT, dtype=jnp.int32)
    positions = jnp.arange(N_DP * N_EXPERT, dtype=jnp.int32)
    counts = jnp.where(positions == chosen, TOK_DEV, counts)
    return counts.reshape(N_DP, N_EXPERT).astype(jnp.int32)


def draw_prev_acts(key, part):
    noise = jax.random.normal(jax.random.fold_in(key, 21), (N_DP, N_EXPERT, GRAD_ROWS, D), jnp.float32)
    values = noise
    return jnp.clip(values, -6.0, 6.0).astype(jnp.bfloat16)


def draw_tokens(key, part):
    noise = jax.random.normal(jax.random.fold_in(key, 22), (N_DP, N_EXPERT, TOK_DEV, D), jnp.float32)
    values = noise
    return jnp.clip(values, -6.0, 6.0).astype(jnp.bfloat16)


def levels(own_key, extent, shards, smallest, largest):
    gain, own = 1.0, jax.random.fold_in(own_key, 6)
    for axis_at, parts in shards:
        draws = jnp.exp(jax.random.uniform(jax.random.fold_in(own, axis_at), (parts,), jnp.float32, smallest / len(shards), largest / len(shards)))
        gain = gain * jnp.repeat(draws, extent[axis_at] // parts).reshape([-1 if axis == axis_at else 1 for axis in range(len(extent))])
    return gain


def assign_block(own_key, own, number, rows, amount, top, most, lean):
    order = jax.random.permutation(own_key, amount)
    crowded, common = load_shares(amount, rows * top, most, lean, True), load_shares(amount, rows * top, most, lean, False)
    places = jnp.arange(amount)

    def named(lengths, offset_by):
        used = int((lengths > 0).sum())
        fixed = max(1, used // 4)
        moved = fixed + (places - fixed + offset_by * (used - fixed)) % max(1, amount - fixed)
        return jnp.zeros((amount,), jnp.int32).at[order[jnp.where(places < fixed, places, moved)]].set(jnp.asarray(lengths, jnp.int32))

    lengths = jnp.where(number % 4 == 0, named(crowded, number // 4), named(common, number - number // 4 - 1))
    mixed = jax.random.permutation(jax.random.fold_in(own, 3), amount)
    source_of, receiver = mixed[0:amount // 2 * 2:2], mixed[1:amount // 2 * 2:2]
    room = jnp.minimum(lengths[source_of] - 1, most - lengths[receiver]) // 2
    room = jnp.where((source_of == order[0]) | (receiver == order[0]) | (lengths[receiver] == 0), 0, jnp.maximum(room, 0))
    moved = jax.random.randint(jax.random.fold_in(own, 4), (amount // 2,), 0, 1 << 20) % (room + 1)
    lengths = lengths.at[source_of].add(-moved).at[receiver].add(moved)
    labels = jnp.searchsorted(jnp.cumsum(lengths), jnp.arange(rows * top), side="right").astype(jnp.int32)
    table = labels.reshape(top, rows).T
    table = table[jax.random.permutation(jax.random.fold_in(own, 1), rows)]
    offset_by = jax.random.randint(jax.random.fold_in(own, 2), (rows, 1), 0, top)
    return jnp.take_along_axis(table, (jnp.arange(top)[None, :] + offset_by) % top, axis=1)


def load_shares(number_of, total, most, lean, full):
    loads = [(1 << 20) // math.isqrt(grade ** lean) + 1 for grade in range(1, number_of + 1)]
    largest = most if full else min(most, max(-(-total // number_of), total * loads[0] // sum(loads)))
    least = 1 if total - largest >= number_of - 1 else 0
    given, spare = [largest] + [least] * (number_of - 1), total - largest - least * (number_of - 1)
    while spare > 0:
        candidates = [i for i in range(1, number_of) if given[i] < largest] or [i for i in range(1, number_of) if given[i] < most]
        pool, remaining = sum([loads[i] for i in candidates]), spare
        for i in candidates:
            extra = min(most - given[i], max(1, remaining * loads[i] // pool), spare)
            given[i] = given[i] + extra
            spare = spare - extra
    return np.array(given)


def centred(rng, extent, deviation, most, split=(), held_as=jnp.bfloat16):
    array = jax.random.normal(rng, extent, jnp.float32) * deviation
    if len(split) > 0:
        array = levels(rng, extent, split, -0.22, 0.18) * array
    return jnp.clip(array, min=-most, max=most).astype(held_as)


def setup_inputs(seed: int = 0) -> dict:
    splits = jax.random.split(jax.random.key(seed), 12)
    prev_acts = draw_prev_acts(jax.random.fold_in(splits[11], 71), 0)
    prev_cot = centred(splits[1], (N_DP, N_EXPERT, GRAD_ROWS, 2 * HID), 0.1, 0.59765625, ((0, 4), (1, 64)))
    weights = centred(splits[2], (N_EXPERT, D, 2 * HID), D ** -0.5, 0.09375, ((0, 64), (1, 4)))
    first_moment = centred(splits[3], (N_EXPERT, D, 2 * HID), 0.3, 1.8, ((0, 64), (1, 4)), jnp.float32)
    second_moment = jnp.clip(jnp.exp(math.log(2.0) - 2.9957323 * jax.random.uniform(splits[4], (N_EXPERT, D, 2 * HID), jnp.float32) ** levels(splits[4], (N_EXPERT, D, 2 * HID), ((0, 64), (1, 4)), -0.2, 0.2)), 0.1, 2.0)
    tokens = draw_tokens(jax.random.fold_in(splits[11], 71), 0)
    routing_keys = jax.random.split(jax.random.fold_in(splits[6], 1), N_DP * N_EXPERT * TOK_DEV // TOK_DEV)
    routing_turns = jax.random.permutation(jax.random.fold_in(splits[6], 3), N_DP * N_EXPERT * TOK_DEV // TOK_DEV)
    routing = jax.vmap(lambda own, number: assign_block(jax.random.fold_in(splits[6], 2), own, number, TOK_DEV, HOT, TOPH, CAP, 2))(routing_keys, routing_turns).reshape((N_DP, N_EXPERT, TOK_DEV, TOPH))
    gates = jnp.clip(0.19921875 + 0.80078125 * jax.random.uniform(splits[7], (N_DP, N_EXPERT, TOK_DEV, TOPH), jnp.float32) ** levels(splits[7], (N_DP, N_EXPERT, TOK_DEV, TOPH), ((0, 4), (1, 64)), -0.2, 0.2), 0.19921875, 1.0).astype(jnp.bfloat16)
    token_counts = draw_token_counts(jax.random.fold_in(splits[11], 71), 0)
    old_owner = jax.random.permutation(splits[9], HOT).astype(jnp.int32)
    new_owner = jax.random.permutation(splits[10], HOT).astype(jnp.int32)
    return {"prev_acts": prev_acts, "prev_cot": prev_cot, "weights": weights, "first_moment": first_moment, "second_moment": second_moment, "tokens": tokens, "routing": routing, "gates": gates, "token_counts": token_counts, "old_owner": old_owner, "new_owner": new_owner}


beta_first = 0.9
beta_second = 0.95
learning = 0.00022
decay_rate = 0.1
epsilon = 1e-08
first_fix = 1.0 - 0.9 ** 40
second_fix = 1.0 - 0.95 ** 40

def adamw(weight_now, first_now, second_now, gradient):
    first_next = beta_first * first_now + (1.0 - beta_first) * gradient
    second_next = beta_second * second_now + (1.0 - beta_second) * gradient * gradient
    stepped = weight_now.astype(jnp.float32) * (1.0 - learning * decay_rate) - learning * (first_next / first_fix) / (jnp.sqrt(second_next / second_fix) + epsilon)
    return (stepped.astype(jnp.bfloat16), first_next, second_next)

def pack_tokens(token_block, route_block, gate_block, limit):
    hot_index = jnp.arange(HOT, dtype=jnp.int32)
    valid = jnp.arange(token_block.shape[0], dtype=jnp.int32) < limit
    hits = (route_block[:, :, None] == hot_index[None, None, :]) & valid[:, None, None]
    named = lax.optimization_barrier(jnp.sum(hits.astype(jnp.int32), axis=1)).astype(jnp.int32)
    scales = lax.optimization_barrier(jnp.sum(jnp.where(hits, gate_block.astype(jnp.float32)[:, :, None], 0.0), axis=1))
    ranks = (jnp.cumsum(named, axis=0) - named).astype(jnp.int32)
    slots = jnp.arange(CAP, dtype=jnp.int32)
    placed = (ranks.T[:, None, :] == slots[None, :, None]) & (named.T[:, None, :] == 1)
    packed = jnp.einsum('hct,td->hcd', placed.astype(jnp.float32), token_block.astype(jnp.float32)).astype(jnp.bfloat16)
    gate_scale = jnp.einsum('hct,th->hc', placed.astype(jnp.float32), scales).astype(jnp.bfloat16)
    return (packed, gate_scale)

def reference(prev_acts, prev_cot, weights, first_moment, second_moment, tokens, routing, gates, token_counts, old_owner, new_owner):
    hot_index = jnp.arange(HOT, dtype=jnp.int32)
    holder = lax.optimization_barrier(jnp.sum(jnp.where(new_owner[None, :] == hot_index[:, None], hot_index[None, :], 0), axis=1)).astype(jnp.int32)
    owners = jnp.arange(N_EXPERT, dtype=jnp.int32)
    source = (jnp.take(old_owner, jnp.take(holder, owners // GRP)) * GRP + owners % GRP).astype(jnp.int32)

    def update(expert):
        running = jnp.zeros((D, 2 * HID), jnp.float32)
        for replica in range(N_DP):
            term = jnp.dot(prev_acts[replica, expert].T, prev_cot[replica, expert], preferred_element_type=jnp.float32)
            running = running + lax.optimization_barrier(term.astype(jnp.bfloat16)).astype(jnp.float32)
        return adamw(weights[expert], first_moment[expert], second_moment[expert], running)
    updated, first_next, second_next = lax.map(update, owners)
    new_weights = jnp.take(updated, source, axis=0)
    new_first = jnp.take(first_next, source, axis=0)
    new_second = jnp.take(second_next, source, axis=0)

    def pack_one(flat_index):
        replica = flat_index // N_EXPERT
        expert = flat_index % N_EXPERT
        return pack_tokens(tokens[replica, expert], routing[replica, expert], gates[replica, expert], token_counts[replica, expert])
    packed, gate_scale = lax.map(pack_one, jnp.arange(N_DP * N_EXPERT, dtype=jnp.int32))
    packed = packed.reshape(N_DP, N_EXPERT, HOT, CAP, D)
    gate_scale = gate_scale.reshape(N_DP, N_EXPERT, HOT, CAP)

    def serve(flat_index):
        replica = flat_index // N_EXPERT
        expert = flat_index % N_EXPERT
        chosen = holder[expert // GRP]
        received = packed[replica][:, chosen].reshape(N_EXPERT * CAP, D)
        scaling = gate_scale[replica][:, chosen].reshape(N_EXPERT * CAP)
        projected = jnp.dot(received, new_weights[expert], preferred_element_type=jnp.float32)
        result = jax.nn.silu(projected[:, :HID]) * projected[:, HID:] * scaling.astype(jnp.float32)[:, None]
        return result.astype(jnp.bfloat16)
    hidden = lax.map(serve, jnp.arange(N_DP * N_EXPERT, dtype=jnp.int32))
    hidden = hidden.reshape(N_DP, N_EXPERT, N_EXPERT * CAP, HID)
    return (hidden, new_weights, new_first, new_second)
```

```python
import jax
import jax.numpy as jnp
from jax import lax
from jax.sharding import Mesh
from jax.sharding import PartitionSpec as P

D = 3584
GRP = 4
SCALE_PAD = 128


beta_first = 0.9
beta_second = 0.95
learning = 0.00022
decay_rate = 0.1
epsilon = 1e-08
first_fix = 1.0 - 0.9**40
second_fix = 1.0 - 0.95**40


def adamw(weight_now, first_now, second_now, gradient):
    first_next = beta_first * first_now + (1.0 - beta_first) * gradient
    second_next = beta_second * second_now + (1.0 - beta_second) * gradient * gradient
    stepped = weight_now.astype(jnp.float32) * (1.0 - learning * decay_rate) - learning * (
        first_next / first_fix
    ) / (jnp.sqrt(second_next / second_fix) + epsilon)
    return stepped.astype(jnp.bfloat16), first_next, second_next


def migrate(state, group_source, groups):
    layers, rows_dev, width = state.shape
    piece_rows = rows_dev // groups
    split = state.reshape(layers, groups, piece_rows, width)
    spread = lax.all_to_all(split, "grp", split_axis=1, concat_axis=1, tiled=True)
    chosen = jnp.take(spread, group_source, axis=1)
    home = lax.all_to_all(chosen, "grp", split_axis=1, concat_axis=1, tiled=True)
    return home.reshape(layers, rows_dev, width)


def pack_tokens(token_block, route_block, gate_block, limit, hot_count, capacity):
    hot_index = jnp.arange(hot_count, dtype=jnp.int32)
    valid = jnp.arange(token_block.shape[0], dtype=jnp.int32) < limit
    hits = (route_block[:, :, None] == hot_index[None, None, :]) & valid[:, None, None]
    named = jnp.sum(hits.astype(jnp.int32), axis=1)
    scales = jnp.sum(jnp.where(hits, gate_block.astype(jnp.float32)[:, :, None], 0.0), axis=1)
    ranks = jnp.cumsum(named, axis=0) - named
    slots = jnp.arange(capacity, dtype=jnp.int32)
    placed = (ranks.T[:, None, :] == slots[None, :, None]) & (named.T[:, None, :] == 1)
    packed = jnp.einsum(
        "hct,td->hcd", placed.astype(jnp.bfloat16), token_block, preferred_element_type=jnp.float32
    ).astype(jnp.bfloat16)
    gate_scale = jnp.einsum("hct,th->hc", placed.astype(jnp.float32), scales).astype(jnp.bfloat16)
    return (packed, gate_scale)


def local(
    prev_acts,
    prev_cot,
    weights,
    first_moment,
    second_moment,
    tokens,
    routing,
    gates,
    token_counts,
    old_owner,
    new_owner,
):
    groups = lax.axis_size("grp")
    per_group = lax.axis_size("pos")
    experts = groups * per_group
    token_slots = tokens.shape[2]
    capacity = min(token_slots, 3 * token_slots // groups)
    width = weights.shape[2]
    hidden_units = width // 2
    activations = prev_acts[0, 0]
    cotangent = prev_cot[0, 0]
    hot_index = jnp.arange(groups, dtype=jnp.int32)
    holder = jnp.sum(
        jnp.where(new_owner[None, :] == hot_index[:, None], hot_index[None, :], 0), axis=1
    )
    group_source = jnp.take(old_owner, holder)

    packed, gate_scale = pack_tokens(
        tokens[0, 0], routing[0, 0], gates[0, 0], token_counts[0, 0], groups, capacity
    )
    scale_cols = jnp.zeros((groups, capacity, SCALE_PAD), jnp.bfloat16).at[:, :, 0].set(gate_scale)
    payload = jnp.concatenate([packed, scale_cols], axis=2)
    to_group = jnp.take(payload, holder, axis=0)
    by_group = lax.all_to_all(to_group, "grp", split_axis=0, concat_axis=0, tiled=True)
    received = lax.all_gather(by_group, "pos", axis=0, tiled=False)

    grads = lax.psum_scatter(
        lax.dot_general(
            activations, cotangent, (((0,), (0,)), ((), ())), preferred_element_type=jnp.float32
        ).astype(jnp.bfloat16),
        "dp",
        scatter_dimension=0,
        tiled=True,
    ).astype(jnp.float32)
    stepped, first_next, second_next = adamw(weights[0], first_moment[0], second_moment[0], grads)
    state = jnp.stack(
        [stepped, first_next.astype(jnp.bfloat16), second_next.astype(jnp.bfloat16)]
    )
    moved = migrate(state, group_source, groups)
    new_weight = moved[0]

    token_rows = received[:, :, :, :D].reshape(experts * capacity, D)
    scaling = received[:, :, :, D].reshape(experts * capacity).astype(jnp.float32)
    projected = jnp.dot(
        token_rows,
        lax.all_gather(new_weight, "dp", axis=0, tiled=True),
        preferred_element_type=jnp.float32,
    )
    result = (
        jax.nn.silu(projected[:, :hidden_units]) * projected[:, hidden_units:] * scaling[:, None]
    )
    hidden = result.astype(jnp.bfloat16).reshape(per_group, groups, capacity, hidden_units)
    hidden = jnp.transpose(hidden, (1, 0, 2, 3)).reshape(1, 1, experts * capacity, hidden_units)
    return (
        hidden,
        new_weight[None],
        moved[1].astype(jnp.float32)[None],
        moved[2].astype(jnp.float32)[None],
    )


def solution(mesh):
    n_dp = mesh.shape["dp"]
    n_expert = mesh.shape["expert"]
    mesh3 = Mesh(
        mesh.devices.reshape(n_dp, n_expert // GRP, GRP), ("dp", "grp", "pos")
    )
    ex = ("grp", "pos")
    in_specs = (
        P("dp", ex, None, None),
        P("dp", ex, None, None),
        P(ex, "dp", None),
        P(ex, "dp", None),
        P(ex, "dp", None),
        P("dp", ex, None, None),
        P("dp", ex, None, None),
        P("dp", ex, None, None),
        P("dp", ex),
        P(),
        P(),
    )
    out_specs = (
        P("dp", ex, None, None),
        P(ex, "dp", None),
        P(ex, "dp", None),
        P(ex, "dp", None),
    )
    return jax.shard_map(local, mesh=mesh3, in_specs=in_specs, out_specs=out_specs, check_vma=False)
```

```python
import jax
import jax.numpy as jnp
from jax import lax
from jax.sharding import Mesh
from jax.sharding import PartitionSpec as P

D = 3584
GRP = 4
SCALE_PAD = 128


beta_first = 0.9
beta_second = 0.95
learning = 0.00022
decay_rate = 0.1
epsilon = 1e-08
first_fix = 1.0 - 0.9**40
second_fix = 1.0 - 0.95**40


def adamw(weight_now, first_now, second_now, gradient):
    first_next = beta_first * first_now + (1.0 - beta_first) * gradient
    second_next = beta_second * second_now + (1.0 - beta_second) * gradient * gradient
    stepped = weight_now.astype(jnp.float32) * (1.0 - learning * decay_rate) - learning * (
        first_next / first_fix
    ) / (jnp.sqrt(second_next / second_fix) + epsilon)
    return stepped.astype(jnp.bfloat16), first_next, second_next


def migrate(state, group_source, groups):
    layers, rows_dev, width = state.shape
    piece_rows = rows_dev // groups
    split = state.reshape(layers, groups, piece_rows, width)
    spread = lax.all_to_all(split, "grp", split_axis=1, concat_axis=1, tiled=True)
    chosen = jnp.take(spread, group_source, axis=1)
    home = lax.all_to_all(chosen, "grp", split_axis=1, concat_axis=1, tiled=True)
    return home.reshape(layers, rows_dev, width)


def pack_tokens(token_block, route_block, gate_block, limit, hot_count, capacity):
    hot_index = jnp.arange(hot_count, dtype=jnp.int32)
    valid = jnp.arange(token_block.shape[0], dtype=jnp.int32) < limit
    hits = (route_block[:, :, None] == hot_index[None, None, :]) & valid[:, None, None]
    named = jnp.sum(hits.astype(jnp.int32), axis=1)
    scales = jnp.sum(jnp.where(hits, gate_block.astype(jnp.float32)[:, :, None], 0.0), axis=1)
    ranks = jnp.cumsum(named, axis=0) - named
    slots = jnp.arange(capacity, dtype=jnp.int32)
    placed = (ranks.T[:, None, :] == slots[None, :, None]) & (named.T[:, None, :] == 1)
    packed = jnp.einsum(
        "hct,td->hcd", placed.astype(jnp.bfloat16), token_block, preferred_element_type=jnp.float32
    ).astype(jnp.bfloat16)
    gate_scale = jnp.einsum("hct,th->hc", placed.astype(jnp.float32), scales).astype(jnp.bfloat16)
    return (packed, gate_scale)


def local(
    prev_acts,
    prev_cot,
    weights,
    first_moment,
    second_moment,
    tokens,
    routing,
    gates,
    token_counts,
    old_owner,
    new_owner,
):
    groups = lax.axis_size("grp")
    experts = groups * GRP
    token_slots = tokens.shape[2]
    capacity = min(token_slots, 3 * token_slots // groups)
    width = weights.shape[2]
    hidden_units = width // 2
    activations = prev_acts[0, 0]
    cotangent = prev_cot[0, 0]
    hot_index = jnp.arange(groups, dtype=jnp.int32)
    holder = jnp.sum(
        jnp.where(new_owner[None, :] == hot_index[:, None], hot_index[None, :], 0), axis=1
    )
    group_source = jnp.take(old_owner, holder)

    packed, gate_scale = pack_tokens(
        tokens[0, 0], routing[0, 0], gates[0, 0], token_counts[0, 0], groups, capacity
    )
    scale_cols = jnp.zeros((groups, capacity, SCALE_PAD), jnp.bfloat16).at[:, :, 0].set(gate_scale)
    payload = jnp.concatenate([packed, scale_cols], axis=2)
    to_group = jnp.take(payload, holder, axis=0)
    by_group = lax.all_to_all(to_group, "grp", split_axis=0, concat_axis=0, tiled=True)
    from_ylo = lax.ppermute(by_group, "ylo", perm=[(0, 1), (1, 0)])
    near = jnp.stack([by_group, from_ylo]).reshape(2 * groups * capacity, D + SCALE_PAD)

    grads = lax.psum_scatter(
        lax.dot_general(
            activations, cotangent, (((0,), (0,)), ((), ())), preferred_element_type=jnp.float32
        ).astype(jnp.bfloat16),
        "dp",
        scatter_dimension=0,
        tiled=True,
    ).astype(jnp.float32)
    stepped, first_next, second_next = adamw(weights[0], first_moment[0], second_moment[0], grads)
    state = jnp.stack(
        [stepped, first_next.astype(jnp.bfloat16), second_next.astype(jnp.bfloat16)]
    )
    moved = migrate(state, group_source, groups)
    new_weight = moved[0]

    partner_weight = lax.ppermute(new_weight, "xhi", perm=[(0, 1), (1, 0)])
    both = lax.all_gather(jnp.stack([new_weight, partner_weight]), "dp", axis=1, tiled=True)
    both = jnp.pad(both, ((0, 0), (0, SCALE_PAD), (0, 0)))
    projected = jnp.einsum("rd,kdn->krn", near, both, preferred_element_type=jnp.float32)
    scaling = near[:, D].astype(jnp.float32)
    result = (
        jax.nn.silu(projected[:, :, :hidden_units])
        * projected[:, :, hidden_units:]
        * scaling[None, :, None]
    ).astype(jnp.bfloat16)
    for_partner = lax.ppermute(result[1], "xhi", perm=[(0, 1), (1, 0)])
    mine = jnp.stack([result[0], for_partner]).reshape(2, 2, groups, capacity, hidden_units)
    ylo = lax.axis_index("ylo")
    xhi = lax.axis_index("xhi")
    flip = jnp.arange(2, dtype=jnp.int32)
    mine = jnp.take(mine, flip ^ xhi, axis=0)
    mine = jnp.take(mine, flip ^ ylo, axis=1)
    hidden = jnp.transpose(mine, (2, 1, 0, 3, 4)).reshape(1, 1, experts * capacity, hidden_units)
    return (
        hidden,
        new_weight[None],
        moved[1].astype(jnp.float32)[None],
        moved[2].astype(jnp.float32)[None],
    )


def solution(mesh):
    n_dp = mesh.shape["dp"]
    n_expert = mesh.shape["expert"]
    mesh4 = Mesh(
        mesh.devices.reshape(n_dp, n_expert // GRP, 2, 2), ("dp", "grp", "ylo", "xhi")
    )
    ex = ("grp", "ylo", "xhi")
    in_specs = (
        P("dp", ex, None, None),
        P("dp", ex, None, None),
        P(ex, "dp", None),
        P(ex, "dp", None),
        P(ex, "dp", None),
        P("dp", ex, None, None),
        P("dp", ex, None, None),
        P("dp", ex, None, None),
        P("dp", ex),
        P(),
        P(),
    )
    out_specs = (
        P("dp", ex, None, None),
        P(ex, "dp", None),
        P(ex, "dp", None),
        P(ex, "dp", None),
    )
    return jax.shard_map(local, mesh=mesh4, in_specs=in_specs, out_specs=out_specs, check_vma=False)
```

```python
import jax
import jax.numpy as jnp
from jax import lax
from jax.sharding import Mesh
from jax.sharding import PartitionSpec as P

D = 3584
GRP = 4
SCALE_PAD = 128


beta_first = 0.9
beta_second = 0.95
learning = 0.00022
decay_rate = 0.1
epsilon = 1e-08
first_fix = 1.0 - 0.9**40
second_fix = 1.0 - 0.95**40


def adamw(weight_now, first_now, second_now, gradient):
    first_next = beta_first * first_now + (1.0 - beta_first) * gradient
    second_next = beta_second * second_now + (1.0 - beta_second) * gradient * gradient
    stepped = weight_now.astype(jnp.float32) * (1.0 - learning * decay_rate) - learning * (
        first_next / first_fix
    ) / (jnp.sqrt(second_next / second_fix) + epsilon)
    return stepped.astype(jnp.bfloat16), first_next, second_next


def migrate(state, group_source, groups):
    layers, rows_dev, width = state.shape
    piece_rows = rows_dev // groups
    split = state.reshape(layers, groups, piece_rows, width)
    spread = lax.all_to_all(split, "grp", split_axis=1, concat_axis=1, tiled=True)
    chosen = jnp.take(spread, group_source, axis=1)
    home = lax.all_to_all(chosen, "grp", split_axis=1, concat_axis=1, tiled=True)
    return home.reshape(layers, rows_dev, width)


def pack_tokens(token_block, route_block, gate_block, limit, hot_count, capacity):
    hot_index = jnp.arange(hot_count, dtype=jnp.int32)
    valid = jnp.arange(token_block.shape[0], dtype=jnp.int32) < limit
    hits = (route_block[:, :, None] == hot_index[None, None, :]) & valid[:, None, None]
    named = jnp.sum(hits.astype(jnp.int32), axis=1)
    scales = jnp.sum(jnp.where(hits, gate_block.astype(jnp.float32)[:, :, None], 0.0), axis=1)
    ranks = jnp.cumsum(named, axis=0) - named
    slots = jnp.arange(capacity, dtype=jnp.int32)
    placed = (ranks.T[:, None, :] == slots[None, :, None]) & (named.T[:, None, :] == 1)
    packed = jnp.einsum(
        "hct,td->hcd", placed.astype(jnp.bfloat16), token_block, preferred_element_type=jnp.float32
    ).astype(jnp.bfloat16)
    gate_scale = jnp.einsum("hct,th->hc", placed.astype(jnp.float32), scales).astype(jnp.bfloat16)
    return (packed, gate_scale)


def local(
    prev_acts,
    prev_cot,
    weights,
    first_moment,
    second_moment,
    tokens,
    routing,
    gates,
    token_counts,
    old_owner,
    new_owner,
):
    groups = lax.axis_size("grp")
    experts = groups * GRP
    token_slots = tokens.shape[2]
    capacity = min(token_slots, 3 * token_slots // groups)
    width = weights.shape[2]
    hidden_units = width // 2
    activations = prev_acts[0, 0]
    cotangent = prev_cot[0, 0]
    hot_index = jnp.arange(groups, dtype=jnp.int32)
    holder = jnp.sum(
        jnp.where(new_owner[None, :] == hot_index[:, None], hot_index[None, :], 0), axis=1
    )
    group_source = jnp.take(old_owner, holder)

    packed, gate_scale = pack_tokens(
        tokens[0, 0], routing[0, 0], gates[0, 0], token_counts[0, 0], groups, capacity
    )
    scale_cols = jnp.zeros((groups, capacity, SCALE_PAD), jnp.bfloat16).at[:, :, 0].set(gate_scale)
    payload = jnp.concatenate([packed, scale_cols], axis=2)
    to_group = jnp.take(payload, holder, axis=0)
    by_group = lax.all_to_all(to_group, "grp", split_axis=0, concat_axis=0, tiled=True)

    grads = lax.psum_scatter(
        lax.dot_general(
            activations, cotangent, (((0,), (0,)), ((), ())), preferred_element_type=jnp.float32
        ).astype(jnp.bfloat16),
        "dp",
        scatter_dimension=0,
        tiled=True,
    )
    by_group, grads = lax.optimization_barrier((by_group, grads))
    grads = grads.astype(jnp.float32)
    near = lax.all_gather(by_group, "ylo", axis=0, tiled=False)
    near = near.reshape(2 * groups * capacity, D + SCALE_PAD)
    stepped, first_next, second_next = adamw(weights[0], first_moment[0], second_moment[0], grads)
    state = jnp.stack(
        [stepped, first_next.astype(jnp.bfloat16), second_next.astype(jnp.bfloat16)]
    )
    moved = migrate(state, group_source, groups)
    new_weight = moved[0]

    partner_weight = lax.ppermute(new_weight, "xhi", perm=[(0, 1), (1, 0)])
    both = lax.all_gather(jnp.stack([new_weight, partner_weight]), "dp", axis=1, tiled=True)
    both = jnp.pad(both, ((0, 0), (0, SCALE_PAD), (0, 0)))
    projected = jnp.einsum("rd,kdn->krn", near, both, preferred_element_type=jnp.float32)
    scaling = near[:, D].astype(jnp.float32)
    result = (
        jax.nn.silu(projected[:, :, :hidden_units])
        * projected[:, :, hidden_units:]
        * scaling[None, :, None]
    ).astype(jnp.bfloat16)
    for_partner = lax.ppermute(result[1], "xhi", perm=[(0, 1), (1, 0)])
    mine = jnp.stack([result[0], for_partner]).reshape(2, 2, groups, capacity, hidden_units)
    xhi = lax.axis_index("xhi")
    flip = jnp.arange(2, dtype=jnp.int32)
    mine = jnp.take(mine, flip ^ xhi, axis=0)
    hidden = jnp.transpose(mine, (2, 1, 0, 3, 4)).reshape(1, 1, experts * capacity, hidden_units)
    return (
        hidden,
        new_weight[None],
        moved[1].astype(jnp.float32)[None],
        moved[2].astype(jnp.float32)[None],
    )


def solution(mesh):
    n_dp = mesh.shape["dp"]
    n_expert = mesh.shape["expert"]
    mesh4 = Mesh(
        mesh.devices.reshape(n_dp, n_expert // GRP, 2, 2), ("dp", "grp", "ylo", "xhi")
    )
    ex = ("grp", "ylo", "xhi")
    in_specs = (
        P("dp", ex, None, None),
        P("dp", ex, None, None),
        P(ex, "dp", None),
        P(ex, "dp", None),
        P(ex, "dp", None),
        P("dp", ex, None, None),
        P("dp", ex, None, None),
        P("dp", ex, None, None),
        P("dp", ex),
        P(),
        P(),
    )
    out_specs = (
        P("dp", ex, None, None),
        P(ex, "dp", None),
        P(ex, "dp", None),
        P(ex, "dp", None),
    )
    return jax.shard_map(local, mesh=mesh4, in_specs=in_specs, out_specs=out_specs, check_vma=False)
```

```python
import jax
import jax.numpy as jnp
from jax import lax
from jax.sharding import Mesh
from jax.sharding import PartitionSpec as P

D = 3584
GRP = 4
SCALE_PAD = 128


beta_first = 0.9
beta_second = 0.95
learning = 0.00022
decay_rate = 0.1
epsilon = 1e-08
first_fix = 1.0 - 0.9**40
second_fix = 1.0 - 0.95**40


def adamw(weight_now, first_now, second_now, gradient):
    first_next = beta_first * first_now + (1.0 - beta_first) * gradient
    second_next = beta_second * second_now + (1.0 - beta_second) * gradient * gradient
    stepped = weight_now.astype(jnp.float32) * (1.0 - learning * decay_rate) - learning * (
        first_next / first_fix
    ) / (jnp.sqrt(second_next / second_fix) + epsilon)
    return stepped.astype(jnp.bfloat16), first_next, second_next


def migrate(state, group_source, groups, held):
    layers, rows_dev, width = state.shape
    piece_rows = rows_dev // groups
    split = state.reshape(layers, groups, piece_rows, width)
    spread = lax.all_to_all(split, "grp", split_axis=1, concat_axis=1, tiled=True)
    chosen = jnp.take(spread, group_source, axis=1)
    chosen, _ = lax.optimization_barrier((chosen, held))
    home = lax.all_to_all(chosen, "grp", split_axis=1, concat_axis=1, tiled=True)
    return home.reshape(layers, rows_dev, width)


def pack_tokens(token_block, route_block, gate_block, limit, hot_count, capacity):
    hot_index = jnp.arange(hot_count, dtype=jnp.int32)
    valid = jnp.arange(token_block.shape[0], dtype=jnp.int32) < limit
    hits = (route_block[:, :, None] == hot_index[None, None, :]) & valid[:, None, None]
    named = jnp.sum(hits.astype(jnp.int32), axis=1)
    scales = jnp.sum(jnp.where(hits, gate_block.astype(jnp.float32)[:, :, None], 0.0), axis=1)
    ranks = jnp.cumsum(named, axis=0) - named
    slots = jnp.arange(capacity, dtype=jnp.int32)
    placed = (ranks.T[:, None, :] == slots[None, :, None]) & (named.T[:, None, :] == 1)
    packed = jnp.einsum(
        "hct,td->hcd", placed.astype(jnp.bfloat16), token_block, preferred_element_type=jnp.float32
    ).astype(jnp.bfloat16)
    gate_scale = jnp.einsum("hct,th->hc", placed.astype(jnp.float32), scales).astype(jnp.bfloat16)
    return (packed, gate_scale)


def local(
    prev_acts,
    prev_cot,
    weights,
    first_moment,
    second_moment,
    tokens,
    routing,
    gates,
    token_counts,
    old_owner,
    new_owner,
):
    groups = lax.axis_size("grp")
    experts = groups * GRP
    token_slots = tokens.shape[2]
    capacity = min(token_slots, 3 * token_slots // groups)
    width = weights.shape[2]
    hidden_units = width // 2
    activations = prev_acts[0, 0]
    cotangent = prev_cot[0, 0]
    hot_index = jnp.arange(groups, dtype=jnp.int32)
    holder = jnp.sum(
        jnp.where(new_owner[None, :] == hot_index[:, None], hot_index[None, :], 0), axis=1
    )
    group_source = jnp.take(old_owner, holder)

    packed, gate_scale = pack_tokens(
        tokens[0, 0], routing[0, 0], gates[0, 0], token_counts[0, 0], groups, capacity
    )
    scale_cols = jnp.zeros((groups, capacity, SCALE_PAD), jnp.bfloat16).at[:, :, 0].set(gate_scale)
    payload = jnp.concatenate([packed, scale_cols], axis=2)
    to_group = jnp.take(payload, holder, axis=0)
    by_group = lax.all_to_all(to_group, "grp", split_axis=0, concat_axis=0, tiled=True)

    grads = lax.psum_scatter(
        lax.dot_general(
            activations, cotangent, (((0,), (0,)), ((), ())), preferred_element_type=jnp.float32
        ).astype(jnp.bfloat16),
        ("xlo", "core"),
        scatter_dimension=0,
        tiled=True,
    )
    by_group, grads = lax.optimization_barrier((by_group, grads))
    grads = grads.astype(jnp.float32)
    near = lax.all_gather(by_group, "ylo", axis=0, tiled=False)
    near = near.reshape(2 * groups * capacity, D + SCALE_PAD)
    stepped, first_next, second_next = adamw(weights[0], first_moment[0], second_moment[0], grads)
    state = jnp.stack(
        [stepped, first_next.astype(jnp.bfloat16), second_next.astype(jnp.bfloat16)]
    )
    moved = migrate(state, group_source, groups, near)
    new_weight = moved[0]

    partner_weight = lax.ppermute(new_weight, "xhi", perm=[(0, 1), (1, 0)])
    shards = lax.all_gather(jnp.stack([new_weight, partner_weight]), "xlo", axis=0, tiled=False)
    shards = lax.all_gather(shards, "core", axis=0, tiled=False)
    both = jnp.transpose(shards, (2, 1, 0, 3, 4)).reshape(2, -1, width)
    both = jnp.pad(both, ((0, 0), (0, SCALE_PAD), (0, 0)))
    projected = jnp.einsum("rd,kdn->krn", near, both, preferred_element_type=jnp.float32)
    scaling = near[:, D].astype(jnp.float32)
    result = (
        jax.nn.silu(projected[:, :, :hidden_units])
        * projected[:, :, hidden_units:]
        * scaling[None, :, None]
    ).astype(jnp.bfloat16)
    for_partner = lax.ppermute(result[1], "xhi", perm=[(0, 1), (1, 0)])
    mine = jnp.stack([result[0], for_partner]).reshape(2, 2, groups, capacity, hidden_units)
    xhi = lax.axis_index("xhi")
    flip = jnp.arange(2, dtype=jnp.int32)
    mine = jnp.take(mine, flip ^ xhi, axis=0)
    hidden = jnp.transpose(mine, (2, 1, 0, 3, 4)).reshape(1, 1, experts * capacity, hidden_units)
    return (
        hidden,
        new_weight[None],
        moved[1].astype(jnp.float32)[None],
        moved[2].astype(jnp.float32)[None],
    )


def solution(mesh):
    n_dp = mesh.shape["dp"]
    n_expert = mesh.shape["expert"]
    mesh4 = Mesh(
        mesh.devices.reshape(2, n_dp // 2, n_expert // GRP, 2, 2),
        ("xlo", "core", "grp", "ylo", "xhi"),
    )
    dp = ("xlo", "core")
    ex = ("grp", "ylo", "xhi")
    in_specs = (
        P(dp, ex, None, None),
        P(dp, ex, None, None),
        P(ex, dp, None),
        P(ex, dp, None),
        P(ex, dp, None),
        P(dp, ex, None, None),
        P(dp, ex, None, None),
        P(dp, ex, None, None),
        P(dp, ex),
        P(),
        P(),
    )
    out_specs = (
        P(dp, ex, None, None),
        P(ex, dp, None),
        P(ex, dp, None),
        P(ex, dp, None),
    )
    return jax.shard_map(local, mesh=mesh4, in_specs=in_specs, out_specs=out_specs, check_vma=False)
```

```python
import jax
import jax.numpy as jnp
from jax import lax
from jax.sharding import Mesh
from jax.sharding import PartitionSpec as P

D = 3584
GRP = 4
SCALE_PAD = 128


beta_first = 0.9
beta_second = 0.95
learning = 0.00022
decay_rate = 0.1
epsilon = 1e-08
first_fix = 1.0 - 0.9**40
second_fix = 1.0 - 0.95**40


def adamw(weight_now, first_now, second_now, gradient):
    first_next = beta_first * first_now + (1.0 - beta_first) * gradient
    second_next = beta_second * second_now + (1.0 - beta_second) * gradient * gradient
    stepped = weight_now.astype(jnp.float32) * (1.0 - learning * decay_rate) - learning * (
        first_next / first_fix
    ) / (jnp.sqrt(second_next / second_fix) + epsilon)
    return stepped.astype(jnp.bfloat16), first_next, second_next


def migrate(state, group_source, groups):
    layers, rows_dev, width = state.shape
    piece_rows = rows_dev // groups
    split = state.reshape(layers, groups, piece_rows, width)
    spread = lax.all_to_all(split, "grp", split_axis=1, concat_axis=1, tiled=True)
    chosen = jnp.take(spread, group_source, axis=1)
    home = lax.all_to_all(chosen, "grp", split_axis=1, concat_axis=1, tiled=True)
    return home.reshape(layers, rows_dev, width)


def pack_tokens(token_block, route_block, gate_block, limit, hot_count, capacity):
    hot_index = jnp.arange(hot_count, dtype=jnp.int32)
    valid = jnp.arange(token_block.shape[0], dtype=jnp.int32) < limit
    hits = (route_block[:, :, None] == hot_index[None, None, :]) & valid[:, None, None]
    named = jnp.sum(hits.astype(jnp.int32), axis=1)
    scales = jnp.sum(jnp.where(hits, gate_block.astype(jnp.float32)[:, :, None], 0.0), axis=1)
    ranks = jnp.cumsum(named, axis=0) - named
    slots = jnp.arange(capacity, dtype=jnp.int32)
    placed = (ranks.T[:, None, :] == slots[None, :, None]) & (named.T[:, None, :] == 1)
    packed = jnp.einsum(
        "hct,td->hcd", placed.astype(jnp.bfloat16), token_block, preferred_element_type=jnp.float32
    ).astype(jnp.bfloat16)
    gate_scale = jnp.einsum("hct,th->hc", placed.astype(jnp.float32), scales).astype(jnp.bfloat16)
    return (packed, gate_scale)


def local(
    prev_acts,
    prev_cot,
    weights,
    first_moment,
    second_moment,
    tokens,
    routing,
    gates,
    token_counts,
    old_owner,
    new_owner,
):
    groups = lax.axis_size("grp")
    experts = groups * GRP
    token_slots = tokens.shape[2]
    capacity = min(token_slots, 3 * token_slots // groups)
    width = weights.shape[2]
    hidden_units = width // 2
    activations = prev_acts[0, 0]
    cotangent = prev_cot[0, 0]
    hot_index = jnp.arange(groups, dtype=jnp.int32)
    holder = jnp.sum(
        jnp.where(new_owner[None, :] == hot_index[:, None], hot_index[None, :], 0), axis=1
    )
    group_source = jnp.take(old_owner, holder)

    packed, gate_scale = pack_tokens(
        tokens[0, 0], routing[0, 0], gates[0, 0], token_counts[0, 0], groups, capacity
    )
    scale_cols = jnp.zeros((groups, capacity, SCALE_PAD), jnp.bfloat16).at[:, :, 0].set(gate_scale)
    payload = jnp.concatenate([packed, scale_cols], axis=2)
    to_group = jnp.take(payload, holder, axis=0)
    by_group = lax.all_to_all(to_group, "grp", split_axis=0, concat_axis=0, tiled=True)

    grads = lax.psum_scatter(
        lax.dot_general(
            activations, cotangent, (((0,), (0,)), ((), ())), preferred_element_type=jnp.float32
        ).astype(jnp.bfloat16),
        "dp",
        scatter_dimension=0,
        tiled=True,
    )
    by_group, grads = lax.optimization_barrier((by_group, grads))
    grads = grads.astype(jnp.float32)
    near = lax.all_gather(by_group, "ylo", axis=0, tiled=False)
    near = near.reshape(2 * groups * capacity, D + SCALE_PAD)
    stepped, first_next, second_next = adamw(weights[0], first_moment[0], second_moment[0], grads)
    new_weight = migrate(stepped[None], group_source, groups)[0]
    moments = jnp.stack([first_next.astype(jnp.bfloat16), second_next.astype(jnp.bfloat16)])
    moments, new_weight = lax.optimization_barrier((moments, new_weight))
    moved = migrate(moments, group_source, groups)

    partner_weight = lax.ppermute(new_weight, "xhi", perm=[(0, 1), (1, 0)])
    both = lax.all_gather(jnp.stack([new_weight, partner_weight]), "dp", axis=1, tiled=True)
    both = jnp.pad(both, ((0, 0), (0, SCALE_PAD), (0, 0)))
    projected = jnp.einsum("rd,kdn->krn", near, both, preferred_element_type=jnp.float32)
    scaling = near[:, D].astype(jnp.float32)
    result = (
        jax.nn.silu(projected[:, :, :hidden_units])
        * projected[:, :, hidden_units:]
        * scaling[None, :, None]
    ).astype(jnp.bfloat16)
    for_partner = lax.ppermute(result[1], "xhi", perm=[(0, 1), (1, 0)])
    mine = jnp.stack([result[0], for_partner]).reshape(2, 2, groups, capacity, hidden_units)
    xhi = lax.axis_index("xhi")
    flip = jnp.arange(2, dtype=jnp.int32)
    mine = jnp.take(mine, flip ^ xhi, axis=0)
    hidden = jnp.transpose(mine, (2, 1, 0, 3, 4)).reshape(1, 1, experts * capacity, hidden_units)
    return (
        hidden,
        new_weight[None],
        moved[0].astype(jnp.float32)[None],
        moved[1].astype(jnp.float32)[None],
    )


def solution(mesh):
    n_dp = mesh.shape["dp"]
    n_expert = mesh.shape["expert"]
    mesh4 = Mesh(
        mesh.devices.reshape(n_dp, n_expert // GRP, 2, 2), ("dp", "grp", "ylo", "xhi")
    )
    ex = ("grp", "ylo", "xhi")
    in_specs = (
        P("dp", ex, None, None),
        P("dp", ex, None, None),
        P(ex, "dp", None),
        P(ex, "dp", None),
        P(ex, "dp", None),
        P("dp", ex, None, None),
        P("dp", ex, None, None),
        P("dp", ex, None, None),
        P("dp", ex),
        P(),
        P(),
    )
    out_specs = (
        P("dp", ex, None, None),
        P(ex, "dp", None),
        P(ex, "dp", None),
        P(ex, "dp", None),
    )
    return jax.shard_map(local, mesh=mesh4, in_specs=in_specs, out_specs=out_specs, check_vma=False)
```

```python
import jax
import jax.numpy as jnp
from jax import lax
from jax.sharding import Mesh
from jax.sharding import PartitionSpec as P

D = 3584
GRP = 4
SCALE_PAD = 128


beta_first = 0.9
beta_second = 0.95
learning = 0.00022
decay_rate = 0.1
epsilon = 1e-08
first_fix = 1.0 - 0.9**40
second_fix = 1.0 - 0.95**40


def adamw(weight_now, first_now, second_now, gradient):
    first_next = beta_first * first_now + (1.0 - beta_first) * gradient
    second_next = beta_second * second_now + (1.0 - beta_second) * gradient * gradient
    stepped = weight_now.astype(jnp.float32) * (1.0 - learning * decay_rate) - learning * (
        first_next / first_fix
    ) / (jnp.sqrt(second_next / second_fix) + epsilon)
    return stepped.astype(jnp.bfloat16), first_next, second_next


def migrate(state, group_source, groups):
    layers, rows_dev, width = state.shape
    piece_rows = rows_dev // groups
    split = state.reshape(layers, groups, piece_rows, width)
    spread = lax.all_to_all(split, "grp", split_axis=1, concat_axis=1, tiled=True)
    chosen = jnp.take(spread, group_source, axis=1)
    home = lax.all_to_all(chosen, "grp", split_axis=1, concat_axis=1, tiled=True)
    return home.reshape(layers, rows_dev, width)


def pack_tokens(token_block, route_block, gate_block, limit, hot_index, capacity):
    valid = jnp.arange(token_block.shape[0], dtype=jnp.int32) < limit
    hits = (route_block[:, :, None] == hot_index[None, None, :]) & valid[:, None, None]
    named = jnp.sum(hits.astype(jnp.int32), axis=1)
    scales = jnp.sum(jnp.where(hits, gate_block.astype(jnp.float32)[:, :, None], 0.0), axis=1)
    ranks = jnp.cumsum(named, axis=0) - named
    slots = jnp.arange(capacity, dtype=jnp.int32)
    placed = (ranks.T[:, None, :] == slots[None, :, None]) & (named.T[:, None, :] == 1)
    packed = jnp.einsum(
        "hct,td->hcd", placed.astype(jnp.bfloat16), token_block, preferred_element_type=jnp.float32
    ).astype(jnp.bfloat16)
    gate_scale = jnp.einsum("hct,th->hc", placed.astype(jnp.float32), scales).astype(jnp.bfloat16)
    return (packed, gate_scale)


def local(
    prev_acts,
    prev_cot,
    weights,
    first_moment,
    second_moment,
    tokens,
    routing,
    gates,
    token_counts,
    old_owner,
    new_owner,
):
    groups = lax.axis_size("grp")
    experts = groups * GRP
    token_slots = tokens.shape[2]
    capacity = min(token_slots, 3 * token_slots // groups)
    width = weights.shape[2]
    hidden_units = width // 2
    activations = prev_acts[0, 0]
    cotangent = prev_cot[0, 0]
    hot_index = jnp.arange(groups, dtype=jnp.int32)
    holder = jnp.sum(
        jnp.where(new_owner[None, :] == hot_index[:, None], hot_index[None, :], 0), axis=1
    )
    group_source = jnp.take(old_owner, holder)

    packed, gate_scale = pack_tokens(
        tokens[0, 0], routing[0, 0], gates[0, 0], token_counts[0, 0], holder, capacity
    )
    scale_cols = jnp.zeros((groups, capacity, SCALE_PAD), jnp.bfloat16).at[:, :, 0].set(gate_scale)
    payload = jnp.concatenate([packed, scale_cols], axis=2)
    by_group = lax.all_to_all(payload, "grp", split_axis=0, concat_axis=0, tiled=True)

    grads = lax.psum_scatter(
        lax.dot_general(
            activations, cotangent, (((0,), (0,)), ((), ())), preferred_element_type=jnp.float32
        ).astype(jnp.bfloat16),
        "dp",
        scatter_dimension=0,
        tiled=True,
    )
    by_group, grads = lax.optimization_barrier((by_group, grads))
    grads = grads.astype(jnp.float32)
    near = lax.all_gather(by_group, "ylo", axis=0, tiled=False)
    near = near.reshape(2 * groups * capacity, D + SCALE_PAD)
    stepped, first_next, second_next = adamw(weights[0], first_moment[0], second_moment[0], grads)
    new_weight = migrate(stepped[None], group_source, groups)[0]
    moments = jnp.stack([first_next.astype(jnp.bfloat16), second_next.astype(jnp.bfloat16)])
    moments, new_weight = lax.optimization_barrier((moments, new_weight))
    moved = migrate(moments, group_source, groups)

    both = lax.all_gather(new_weight, ("xhi", "dp"), axis=0, tiled=True)
    both = both.reshape(2, -1, width)
    both = jnp.pad(both, ((0, 0), (0, SCALE_PAD), (0, 0)))
    projected = jnp.einsum("rd,kdn->krn", near, both, preferred_element_type=jnp.float32)
    scaling = near[:, D].astype(jnp.float32)
    result = (
        jax.nn.silu(projected[:, :, :hidden_units])
        * projected[:, :, hidden_units:]
        * scaling[None, :, None]
    ).astype(jnp.bfloat16)
    xhi = lax.axis_index("xhi")
    own = lax.dynamic_index_in_dim(result, xhi, axis=0, keepdims=False)
    other = lax.dynamic_index_in_dim(result, 1 - xhi, axis=0, keepdims=False)
    for_partner = lax.ppermute(other, "xhi", perm=[(0, 1), (1, 0)])
    mine = jnp.stack([own, for_partner]).reshape(2, 2, groups, capacity, hidden_units)
    flip = jnp.arange(2, dtype=jnp.int32)
    mine = jnp.take(mine, flip ^ xhi, axis=0)
    hidden = jnp.transpose(mine, (2, 1, 0, 3, 4)).reshape(1, 1, experts * capacity, hidden_units)
    return (
        hidden,
        new_weight[None],
        moved[0].astype(jnp.float32)[None],
        moved[1].astype(jnp.float32)[None],
    )


def solution(mesh):
    n_dp = mesh.shape["dp"]
    n_expert = mesh.shape["expert"]
    mesh4 = Mesh(
        mesh.devices.reshape(n_dp, n_expert // GRP, 2, 2), ("dp", "grp", "ylo", "xhi")
    )
    ex = ("grp", "ylo", "xhi")
    in_specs = (
        P("dp", ex, None, None),
        P("dp", ex, None, None),
        P(ex, "dp", None),
        P(ex, "dp", None),
        P(ex, "dp", None),
        P("dp", ex, None, None),
        P("dp", ex, None, None),
        P("dp", ex, None, None),
        P("dp", ex),
        P(),
        P(),
    )
    out_specs = (
        P("dp", ex, None, None),
        P(ex, "dp", None),
        P(ex, "dp", None),
        P(ex, "dp", None),
    )
    return jax.shard_map(local, mesh=mesh4, in_specs=in_specs, out_specs=out_specs, check_vma=False)
```

```python
import jax
import jax.numpy as jnp
from jax import lax
from jax.sharding import Mesh
from jax.sharding import PartitionSpec as P

D = 3584
GRP = 4
SCALE_PAD = 128


beta_first = 0.9
beta_second = 0.95
learning = 0.00022
decay_rate = 0.1
epsilon = 1e-08
first_fix = 1.0 - 0.9**40
second_fix = 1.0 - 0.95**40


def adamw(weight_now, first_now, second_now, gradient):
    first_next = beta_first * first_now + (1.0 - beta_first) * gradient
    second_next = beta_second * second_now + (1.0 - beta_second) * gradient * gradient
    stepped = weight_now.astype(jnp.float32) * (1.0 - learning * decay_rate) - learning * (
        first_next / first_fix
    ) / (jnp.sqrt(second_next / second_fix) + epsilon)
    return stepped.astype(jnp.bfloat16), first_next, second_next


def migrate(state, group_source, groups):
    layers, rows_dev, width = state.shape
    piece_rows = rows_dev // groups
    split = state.reshape(layers, groups, piece_rows, width)
    spread = lax.all_to_all(split, "grp", split_axis=1, concat_axis=1, tiled=True)
    chosen = jnp.take(spread, group_source, axis=1)
    home = lax.all_to_all(chosen, "grp", split_axis=1, concat_axis=1, tiled=True)
    return home.reshape(layers, rows_dev, width)


def pack_tokens(token_block, route_block, gate_block, limit, hot_index, capacity):
    valid = jnp.arange(token_block.shape[0], dtype=jnp.int32) < limit
    hits = (route_block[:, :, None] == hot_index[None, None, :]) & valid[:, None, None]
    named = jnp.sum(hits.astype(jnp.int32), axis=1)
    scales = jnp.sum(jnp.where(hits, gate_block.astype(jnp.float32)[:, :, None], 0.0), axis=1)
    ranks = jnp.cumsum(named, axis=0) - named
    slots = jnp.arange(capacity, dtype=jnp.int32)
    placed = (ranks.T[:, None, :] == slots[None, :, None]) & (named.T[:, None, :] == 1)
    packed = jnp.einsum(
        "hct,td->hcd", placed.astype(jnp.bfloat16), token_block, preferred_element_type=jnp.float32
    ).astype(jnp.bfloat16)
    gate_scale = jnp.einsum("hct,th->hc", placed.astype(jnp.float32), scales).astype(jnp.bfloat16)
    return (packed, gate_scale)


def local(
    prev_acts,
    prev_cot,
    weights,
    first_moment,
    second_moment,
    tokens,
    routing,
    gates,
    token_counts,
    old_owner,
    new_owner,
):
    groups = lax.axis_size("grp")
    experts = groups * GRP
    token_slots = tokens.shape[2]
    capacity = min(token_slots, 3 * token_slots // groups)
    width = weights.shape[2]
    hidden_units = width // 2
    activations = prev_acts[0, 0]
    cotangent = prev_cot[0, 0]
    hot_index = jnp.arange(groups, dtype=jnp.int32)
    holder = jnp.sum(
        jnp.where(new_owner[None, :] == hot_index[:, None], hot_index[None, :], 0), axis=1
    )
    group_source = jnp.take(old_owner, holder)

    packed, gate_scale = pack_tokens(
        tokens[0, 0], routing[0, 0], gates[0, 0], token_counts[0, 0], holder, capacity
    )
    scale_cols = jnp.zeros((groups, capacity, SCALE_PAD), jnp.bfloat16).at[:, :, 0].set(gate_scale)
    payload = jnp.concatenate([packed, scale_cols], axis=2)
    by_group = lax.all_to_all(payload, "grp", split_axis=0, concat_axis=0, tiled=True)

    grads = lax.psum_scatter(
        lax.dot_general(
            activations, cotangent, (((0,), (0,)), ((), ())), preferred_element_type=jnp.float32
        ).astype(jnp.bfloat16),
        "dp",
        scatter_dimension=0,
        tiled=True,
    )
    by_group, grads = lax.optimization_barrier((by_group, grads))
    grads = grads.astype(jnp.float32)
    near = lax.all_gather(by_group, "ylo", axis=0, tiled=False)
    near = near.reshape(2 * groups * capacity, D + SCALE_PAD)
    stepped, first_next, second_next = adamw(weights[0], first_moment[0], second_moment[0], grads)
    new_weight = migrate(stepped[None], group_source, groups)[0]
    moments = jnp.stack([first_next.astype(jnp.bfloat16), second_next.astype(jnp.bfloat16)])
    moments, new_weight = lax.optimization_barrier((moments, new_weight))
    moved = migrate(moments, group_source, groups)

    both = lax.all_gather(new_weight, ("xhi", "dp"), axis=0, tiled=True)
    both = both.reshape(2, -1, width)
    both = jnp.pad(both, ((0, 0), (0, SCALE_PAD), (0, 0)))
    projected = jnp.stack(
        [jnp.dot(near, both[k], preferred_element_type=jnp.float32) for k in range(2)]
    )
    scaling = near[:, D].astype(jnp.float32)
    result = (
        jax.nn.silu(projected[:, :, :hidden_units])
        * projected[:, :, hidden_units:]
        * scaling[None, :, None]
    ).astype(jnp.bfloat16)
    xhi = lax.axis_index("xhi")
    own = lax.dynamic_index_in_dim(result, xhi, axis=0, keepdims=False)
    other = lax.dynamic_index_in_dim(result, 1 - xhi, axis=0, keepdims=False)
    for_partner = lax.ppermute(other, "xhi", perm=[(0, 1), (1, 0)])
    mine = jnp.stack([own, for_partner]).reshape(2, 2, groups, capacity, hidden_units)
    flip = jnp.arange(2, dtype=jnp.int32)
    mine = jnp.take(mine, flip ^ xhi, axis=0)
    hidden = jnp.transpose(mine, (2, 1, 0, 3, 4)).reshape(1, 1, experts * capacity, hidden_units)
    return (
        hidden,
        new_weight[None],
        moved[0].astype(jnp.float32)[None],
        moved[1].astype(jnp.float32)[None],
    )


def solution(mesh):
    n_dp = mesh.shape["dp"]
    n_expert = mesh.shape["expert"]
    mesh4 = Mesh(
        mesh.devices.reshape(n_dp, n_expert // GRP, 2, 2), ("dp", "grp", "ylo", "xhi")
    )
    ex = ("grp", "ylo", "xhi")
    in_specs = (
        P("dp", ex, None, None),
        P("dp", ex, None, None),
        P(ex, "dp", None),
        P(ex, "dp", None),
        P(ex, "dp", None),
        P("dp", ex, None, None),
        P("dp", ex, None, None),
        P("dp", ex, None, None),
        P("dp", ex),
        P(),
        P(),
    )
    out_specs = (
        P("dp", ex, None, None),
        P(ex, "dp", None),
        P(ex, "dp", None),
        P(ex, "dp", None),
    )
    return jax.shard_map(local, mesh=mesh4, in_specs=in_specs, out_specs=out_specs, check_vma=False)
```

```python
import jax
import jax.numpy as jnp
from jax import lax
from jax.sharding import Mesh
from jax.sharding import PartitionSpec as P

D = 3584
GRP = 4
SCALE_PAD = 128


beta_first = 0.9
beta_second = 0.95
learning = 0.00022
decay_rate = 0.1
epsilon = 1e-08
first_fix = 1.0 - 0.9**40
second_fix = 1.0 - 0.95**40


def adamw(weight_now, first_now, second_now, gradient):
    first_next = beta_first * first_now + (1.0 - beta_first) * gradient
    second_next = beta_second * second_now + (1.0 - beta_second) * gradient * gradient
    stepped = weight_now.astype(jnp.float32) * (1.0 - learning * decay_rate) - learning * (
        first_next / first_fix
    ) / (jnp.sqrt(second_next / second_fix) + epsilon)
    return stepped.astype(jnp.bfloat16), first_next, second_next


def migrate(state, group_source, groups):
    layers, rows_dev, width = state.shape
    piece_rows = rows_dev // groups
    split = state.reshape(layers, groups, piece_rows, width)
    spread = lax.all_to_all(split, "grp", split_axis=1, concat_axis=1, tiled=True)
    chosen = jnp.take(spread, group_source, axis=1)
    home = lax.all_to_all(chosen, "grp", split_axis=1, concat_axis=1, tiled=True)
    return home.reshape(layers, rows_dev, width)


def pack_tokens(token_block, route_block, gate_block, limit, hot_index, capacity):
    valid = jnp.arange(token_block.shape[0], dtype=jnp.int32) < limit
    hits = (route_block[:, :, None] == hot_index[None, None, :]) & valid[:, None, None]
    named = jnp.sum(hits.astype(jnp.int32), axis=1)
    scales = jnp.sum(jnp.where(hits, gate_block.astype(jnp.float32)[:, :, None], 0.0), axis=1)
    ranks = jnp.cumsum(named, axis=0) - named
    slots = jnp.arange(capacity, dtype=jnp.int32)
    placed = (ranks.T[:, None, :] == slots[None, :, None]) & (named.T[:, None, :] == 1)
    packed = jnp.einsum(
        "hct,td->hcd", placed.astype(jnp.bfloat16), token_block, preferred_element_type=jnp.float32
    ).astype(jnp.bfloat16)
    gate_scale = jnp.einsum("hct,th->hc", placed.astype(jnp.float32), scales).astype(jnp.bfloat16)
    return (packed, gate_scale)


def local(
    prev_acts,
    prev_cot,
    weights,
    first_moment,
    second_moment,
    tokens,
    routing,
    gates,
    token_counts,
    old_owner,
    new_owner,
):
    groups = lax.axis_size("grp")
    experts = groups * GRP
    token_slots = tokens.shape[2]
    capacity = min(token_slots, 3 * token_slots // groups)
    width = weights.shape[2]
    hidden_units = width // 2
    activations = prev_acts[0, 0]
    cotangent = prev_cot[0, 0]
    hot_index = jnp.arange(groups, dtype=jnp.int32)
    holder = jnp.sum(
        jnp.where(new_owner[None, :] == hot_index[:, None], hot_index[None, :], 0), axis=1
    )
    group_source = jnp.take(old_owner, holder)

    packed, gate_scale = pack_tokens(
        tokens[0, 0], routing[0, 0], gates[0, 0], token_counts[0, 0], holder, capacity
    )
    scale_cols = jnp.zeros((groups, capacity, SCALE_PAD), jnp.bfloat16).at[:, :, 0].set(gate_scale)
    payload = jnp.concatenate([packed, scale_cols], axis=2)
    g = lax.axis_index("grp")
    by_shift = [lax.dynamic_index_in_dim(payload, g, axis=0, keepdims=False)]
    for k in range(1, groups):
        send = lax.dynamic_index_in_dim(payload, (g + k) % groups, axis=0, keepdims=False)
        pairs = [(i, (i + k) % groups) for i in range(groups)]
        by_shift.append(lax.ppermute(send, "grp", perm=pairs))
    by_group = jnp.stack(by_shift)

    grads = lax.psum_scatter(
        lax.dot_general(
            activations, cotangent, (((0,), (0,)), ((), ())), preferred_element_type=jnp.float32
        ).astype(jnp.bfloat16),
        "dp",
        scatter_dimension=0,
        tiled=True,
    )
    by_group, grads = lax.optimization_barrier((by_group, grads))
    grads = grads.astype(jnp.float32)
    near = lax.all_gather(by_group, "ylo", axis=0, tiled=False)
    near = near.reshape(2 * groups * capacity, D + SCALE_PAD)
    stepped, first_next, second_next = adamw(weights[0], first_moment[0], second_moment[0], grads)
    new_weight = migrate(stepped[None], group_source, groups)[0]
    moments = jnp.stack([first_next.astype(jnp.bfloat16), second_next.astype(jnp.bfloat16)])
    moments, new_weight = lax.optimization_barrier((moments, new_weight))
    moved = migrate(moments, group_source, groups)

    both = lax.all_gather(new_weight, ("xhi", "dp"), axis=0, tiled=True)
    both = both.reshape(2, -1, width)
    both = jnp.pad(both, ((0, 0), (0, SCALE_PAD), (0, 0)))
    projected = jnp.stack(
        [jnp.dot(near, both[k], preferred_element_type=jnp.float32) for k in range(2)]
    )
    scaling = near[:, D].astype(jnp.float32)
    result = (
        jax.nn.silu(projected[:, :, :hidden_units])
        * projected[:, :, hidden_units:]
        * scaling[None, :, None]
    ).astype(jnp.bfloat16)
    xhi = lax.axis_index("xhi")
    own = lax.dynamic_index_in_dim(result, xhi, axis=0, keepdims=False)
    other = lax.dynamic_index_in_dim(result, 1 - xhi, axis=0, keepdims=False)
    for_partner = lax.ppermute(other, "xhi", perm=[(0, 1), (1, 0)])
    mine = jnp.stack([own, for_partner]).reshape(2, 2, groups, capacity, hidden_units)
    flip = jnp.arange(2, dtype=jnp.int32)
    mine = jnp.take(mine, flip ^ xhi, axis=0)
    mine = jnp.take(mine, (g - jnp.arange(groups, dtype=jnp.int32)) % groups, axis=2)
    hidden = jnp.transpose(mine, (2, 1, 0, 3, 4)).reshape(1, 1, experts * capacity, hidden_units)
    return (
        hidden,
        new_weight[None],
        moved[0].astype(jnp.float32)[None],
        moved[1].astype(jnp.float32)[None],
    )


def solution(mesh):
    n_dp = mesh.shape["dp"]
    n_expert = mesh.shape["expert"]
    mesh4 = Mesh(
        mesh.devices.reshape(n_dp, n_expert // GRP, 2, 2), ("dp", "grp", "ylo", "xhi")
    )
    ex = ("grp", "ylo", "xhi")
    in_specs = (
        P("dp", ex, None, None),
        P("dp", ex, None, None),
        P(ex, "dp", None),
        P(ex, "dp", None),
        P(ex, "dp", None),
        P("dp", ex, None, None),
        P("dp", ex, None, None),
        P("dp", ex, None, None),
        P("dp", ex),
        P(),
        P(),
    )
    out_specs = (
        P("dp", ex, None, None),
        P(ex, "dp", None),
        P(ex, "dp", None),
        P(ex, "dp", None),
    )
    return jax.shard_map(local, mesh=mesh4, in_specs=in_specs, out_specs=out_specs, check_vma=False)
```

```python
import jax
import jax.numpy as jnp
from jax import lax
from jax.sharding import Mesh
from jax.sharding import PartitionSpec as P

D = 3584
GRP = 4


beta_first = 0.9
beta_second = 0.95
learning = 0.00022
decay_rate = 0.1
epsilon = 1e-08
first_fix = 1.0 - 0.9**40
second_fix = 1.0 - 0.95**40


def adamw(weight_now, first_now, second_now, gradient):
    first_next = beta_first * first_now + (1.0 - beta_first) * gradient
    second_next = beta_second * second_now + (1.0 - beta_second) * gradient * gradient
    stepped = weight_now.astype(jnp.float32) * (1.0 - learning * decay_rate) - learning * (
        first_next / first_fix
    ) / (jnp.sqrt(second_next / second_fix) + epsilon)
    return stepped.astype(jnp.bfloat16), first_next, second_next


def migrate(state, group_source, groups):
    layers, rows_dev, width = state.shape
    piece_rows = rows_dev // groups
    split = state.reshape(layers, groups, piece_rows, width)
    spread = lax.all_to_all(split, "grp", split_axis=1, concat_axis=1, tiled=True)
    chosen = jnp.take(spread, group_source, axis=1, mode="clip", unique_indices=True)
    home = lax.all_to_all(chosen, "grp", split_axis=1, concat_axis=1, tiled=True)
    return home.reshape(layers, rows_dev, width)


def pack_tokens(token_block, route_block, gate_block, limit, hot_index, capacity):
    valid = jnp.arange(token_block.shape[0], dtype=jnp.int32) < limit
    hits = (route_block[:, :, None] == hot_index[None, None, :]) & valid[:, None, None]
    named = jnp.sum(hits.astype(jnp.int32), axis=1)
    scales = jnp.sum(jnp.where(hits, gate_block.astype(jnp.float32)[:, :, None], 0.0), axis=1)
    ranks = jnp.cumsum(named, axis=0) - named
    slots = jnp.arange(capacity, dtype=jnp.int32)
    placed = (ranks.T[:, None, :] == slots[None, :, None]) & (named.T[:, None, :] == 1)
    packed = jnp.einsum(
        "hct,td->hcd", placed.astype(jnp.bfloat16), token_block, preferred_element_type=jnp.float32
    ).astype(jnp.bfloat16)
    gate_scale = jnp.einsum("hct,th->hc", placed.astype(jnp.float32), scales).astype(jnp.bfloat16)
    return (packed, gate_scale)


def local(
    prev_acts,
    prev_cot,
    weights,
    first_moment,
    second_moment,
    tokens,
    routing,
    gates,
    token_counts,
    old_owner,
    new_owner,
):
    groups = lax.axis_size("grp")
    experts = groups * GRP
    token_slots = tokens.shape[2]
    capacity = min(token_slots, 3 * token_slots // groups)
    width = weights.shape[2]
    hidden_units = width // 2
    activations = prev_acts[0, 0]
    cotangent = prev_cot[0, 0]
    hot_index = jnp.arange(groups, dtype=jnp.int32)
    holder = jnp.sum(
        jnp.where(new_owner[None, :] == hot_index[:, None], hot_index[None, :], 0), axis=1
    )
    group_source = jnp.take(old_owner, holder)

    packed, gate_scale = pack_tokens(
        tokens[0, 0], routing[0, 0], gates[0, 0], token_counts[0, 0], holder, capacity
    )
    by_group = lax.all_to_all(packed, "grp", split_axis=0, concat_axis=0, tiled=True)
    all_scales = lax.all_gather(gate_scale, ("grp", "ylo", "xhi"), axis=0, tiled=False)

    grads = lax.psum_scatter(
        lax.dot_general(
            activations, cotangent, (((0,), (0,)), ((), ())), preferred_element_type=jnp.float32
        ).astype(jnp.bfloat16),
        "dp",
        scatter_dimension=0,
        tiled=True,
    )
    by_group, grads = lax.optimization_barrier((by_group, grads))
    grads = grads.astype(jnp.float32)
    near = lax.all_gather(by_group, "ylo", axis=0, tiled=False)
    near = near.reshape(2 * groups * capacity, D)
    stepped, first_next, second_next = adamw(weights[0], first_moment[0], second_moment[0], grads)
    new_weight = migrate(stepped[None], group_source, groups)[0]
    moments = jnp.stack([first_next.astype(jnp.bfloat16), second_next.astype(jnp.bfloat16)])
    moments, new_weight = lax.optimization_barrier((moments, new_weight))
    moved = migrate(moments, group_source, groups)

    both = lax.all_gather(new_weight, ("xhi", "dp"), axis=0, tiled=True)
    both = both.reshape(2, -1, width)
    projected = jnp.stack(
        [jnp.dot(near, both[k], preferred_element_type=jnp.float32) for k in range(2)]
    )
    g = lax.axis_index("grp")
    xhi = lax.axis_index("xhi")
    scales = all_scales.reshape(groups, 2, 2, groups, capacity)
    scales = lax.dynamic_index_in_dim(scales, xhi, axis=2, keepdims=False)
    scales = lax.dynamic_index_in_dim(scales, g, axis=2, keepdims=False)
    scaling = jnp.transpose(scales, (1, 0, 2)).reshape(-1).astype(jnp.float32)
    result = (
        jax.nn.silu(projected[:, :, :hidden_units])
        * projected[:, :, hidden_units:]
        * scaling[None, :, None]
    ).astype(jnp.bfloat16)
    own = lax.dynamic_index_in_dim(result, xhi, axis=0, keepdims=False)
    other = lax.dynamic_index_in_dim(result, 1 - xhi, axis=0, keepdims=False)
    for_partner = lax.ppermute(other, "xhi", perm=[(0, 1), (1, 0)])
    mine = jnp.stack([own, for_partner]).reshape(2, 2, groups, capacity, hidden_units)
    flip = jnp.arange(2, dtype=jnp.int32)
    mine = jnp.take(mine, flip ^ xhi, axis=0)
    hidden = jnp.transpose(mine, (2, 1, 0, 3, 4)).reshape(1, 1, experts * capacity, hidden_units)
    return (
        hidden,
        new_weight[None],
        moved[0].astype(jnp.float32)[None],
        moved[1].astype(jnp.float32)[None],
    )


def solution(mesh):
    n_dp = mesh.shape["dp"]
    n_expert = mesh.shape["expert"]
    mesh4 = Mesh(
        mesh.devices.reshape(n_dp, n_expert // GRP, 2, 2), ("dp", "grp", "ylo", "xhi")
    )
    ex = ("grp", "ylo", "xhi")
    in_specs = (
        P("dp", ex, None, None),
        P("dp", ex, None, None),
        P(ex, "dp", None),
        P(ex, "dp", None),
        P(ex, "dp", None),
        P("dp", ex, None, None),
        P("dp", ex, None, None),
        P("dp", ex, None, None),
        P("dp", ex),
        P(),
        P(),
    )
    out_specs = (
        P("dp", ex, None, None),
        P(ex, "dp", None),
        P(ex, "dp", None),
        P(ex, "dp", None),
    )
    return jax.shard_map(local, mesh=mesh4, in_specs=in_specs, out_specs=out_specs, check_vma=False)
```

```python
import jax
import jax.numpy as jnp
from jax import lax
from jax.sharding import Mesh
from jax.sharding import PartitionSpec as P

D = 3584
GRP = 4
SCALE_PAD = 128


beta_first = 0.9
beta_second = 0.95
learning = 0.00022
decay_rate = 0.1
epsilon = 1e-08
first_fix = 1.0 - 0.9**40
second_fix = 1.0 - 0.95**40


def adamw(weight_now, first_now, second_now, gradient):
    first_next = beta_first * first_now + (1.0 - beta_first) * gradient
    second_next = beta_second * second_now + (1.0 - beta_second) * gradient * gradient
    stepped = weight_now.astype(jnp.float32) * (1.0 - learning * decay_rate) - learning * (
        first_next / first_fix
    ) / (jnp.sqrt(second_next / second_fix) + epsilon)
    return stepped.astype(jnp.bfloat16), first_next, second_next


def migrate(state, group_source, groups):
    layers, rows_dev, width = state.shape
    piece_rows = rows_dev // groups
    split = state.reshape(layers, groups, piece_rows, width)
    spread = lax.all_to_all(split, "grp", split_axis=1, concat_axis=1, tiled=True)
    chosen = jnp.take(spread, group_source, axis=1, mode="clip", unique_indices=True)
    home = lax.all_to_all(chosen, "grp", split_axis=1, concat_axis=1, tiled=True)
    return home.reshape(layers, rows_dev, width)


def pack_tokens(token_block, route_block, gate_block, limit, hot_index, capacity):
    valid = jnp.arange(token_block.shape[0], dtype=jnp.int32) < limit
    hits = (route_block[:, :, None] == hot_index[None, None, :]) & valid[:, None, None]
    named = jnp.sum(hits.astype(jnp.int32), axis=1)
    scales = jnp.sum(jnp.where(hits, gate_block.astype(jnp.float32)[:, :, None], 0.0), axis=1)
    ranks = jnp.cumsum(named, axis=0) - named
    slots = jnp.arange(capacity, dtype=jnp.int32)
    placed = (ranks.T[:, None, :] == slots[None, :, None]) & (named.T[:, None, :] == 1)
    packed = jnp.einsum(
        "hct,td->hcd", placed.astype(jnp.bfloat16), token_block, preferred_element_type=jnp.float32
    ).astype(jnp.bfloat16)
    gate_scale = jnp.einsum("hct,th->hc", placed.astype(jnp.float32), scales).astype(jnp.bfloat16)
    return (packed, gate_scale)


def local(
    prev_acts,
    prev_cot,
    weights,
    first_moment,
    second_moment,
    tokens,
    routing,
    gates,
    token_counts,
    old_owner,
    new_owner,
):
    groups = lax.axis_size("grp")
    experts = groups * GRP
    token_slots = tokens.shape[2]
    capacity = min(token_slots, 3 * token_slots // groups)
    width = weights.shape[2]
    hidden_units = width // 2
    activations = prev_acts[0, 0]
    cotangent = prev_cot[0, 0]
    hot_index = jnp.arange(groups, dtype=jnp.int32)
    holder = jnp.sum(
        jnp.where(new_owner[None, :] == hot_index[:, None], hot_index[None, :], 0), axis=1
    )
    group_source = jnp.take(old_owner, holder)

    packed, gate_scale = pack_tokens(
        tokens[0, 0], routing[0, 0], gates[0, 0], token_counts[0, 0], holder, capacity
    )
    scale_cols = jnp.zeros((groups, capacity, SCALE_PAD), jnp.bfloat16).at[:, :, 0].set(gate_scale)
    payload = jnp.concatenate([packed, scale_cols], axis=2)
    by_group = lax.all_to_all(payload, "grp", split_axis=0, concat_axis=0, tiled=True)

    grads = lax.psum_scatter(
        lax.dot_general(
            activations, cotangent, (((0,), (0,)), ((), ())), preferred_element_type=jnp.float32
        ).astype(jnp.bfloat16),
        "dp",
        scatter_dimension=0,
        tiled=True,
    )
    by_group, grads = lax.optimization_barrier((by_group, grads))
    grads = grads.astype(jnp.float32)
    near = lax.all_gather(by_group, "ylo", axis=0, tiled=False)
    near = near.reshape(2 * groups * capacity, D + SCALE_PAD)
    stepped, first_next, second_next = adamw(weights[0], first_moment[0], second_moment[0], grads)
    new_weight = migrate(stepped[None], group_source, groups)[0]
    moments = jnp.stack([first_next.astype(jnp.bfloat16), second_next.astype(jnp.bfloat16)])
    moments, new_weight = lax.optimization_barrier((moments, new_weight))
    moved = migrate(moments, group_source, groups)

    both = lax.all_gather(new_weight, ("xhi", "dp"), axis=0, tiled=True)
    both = both.reshape(2, -1, width)
    both = jnp.pad(both, ((0, 0), (0, SCALE_PAD), (0, 0)))
    projected = jnp.stack(
        [jnp.dot(near, both[k], preferred_element_type=jnp.float32) for k in range(2)]
    )
    scaling = near[:, D].astype(jnp.float32)
    result = (
        jax.nn.silu(projected[:, :, :hidden_units])
        * projected[:, :, hidden_units:]
        * scaling[None, :, None]
    ).astype(jnp.bfloat16)
    xhi = lax.axis_index("xhi")
    own = lax.dynamic_index_in_dim(result, xhi, axis=0, keepdims=False)
    other = lax.dynamic_index_in_dim(result, 1 - xhi, axis=0, keepdims=False)
    for_partner = lax.ppermute(other, "xhi", perm=[(0, 1), (1, 0)])
    mine = jnp.stack([own, for_partner]).reshape(2, 2, groups, capacity, hidden_units)
    flip = jnp.arange(2, dtype=jnp.int32)
    mine = jnp.take(mine, flip ^ xhi, axis=0)
    hidden = jnp.transpose(mine, (2, 1, 0, 3, 4)).reshape(1, 1, experts * capacity, hidden_units)
    return (
        hidden,
        new_weight[None],
        moved[0].astype(jnp.float32)[None],
        moved[1].astype(jnp.float32)[None],
    )


def solution(mesh):
    n_dp = mesh.shape["dp"]
    n_expert = mesh.shape["expert"]
    mesh4 = Mesh(
        mesh.devices.reshape(n_dp, n_expert // GRP, 2, 2), ("dp", "grp", "ylo", "xhi")
    )
    ex = ("grp", "ylo", "xhi")
    in_specs = (
        P("dp", ex, None, None),
        P("dp", ex, None, None),
        P(ex, "dp", None),
        P(ex, "dp", None),
        P(ex, "dp", None),
        P("dp", ex, None, None),
        P("dp", ex, None, None),
        P("dp", ex, None, None),
        P("dp", ex),
        P(),
        P(),
    )
    out_specs = (
        P("dp", ex, None, None),
        P(ex, "dp", None),
        P(ex, "dp", None),
        P(ex, "dp", None),
    )
    return jax.shard_map(local, mesh=mesh4, in_specs=in_specs, out_specs=out_specs, check_vma=False)
```

```python
import jax
import jax.numpy as jnp
from jax import lax
from jax.sharding import Mesh
from jax.sharding import PartitionSpec as P

D = 3584
GRP = 4
SCALE_PAD = 128


beta_first = 0.9
beta_second = 0.95
learning = 0.00022
decay_rate = 0.1
epsilon = 1e-08
first_fix = 1.0 - 0.9**40
second_fix = 1.0 - 0.95**40


def adamw(weight_now, first_now, second_now, gradient):
    first_next = beta_first * first_now + (1.0 - beta_first) * gradient
    second_next = beta_second * second_now + (1.0 - beta_second) * gradient * gradient
    stepped = weight_now.astype(jnp.float32) * (1.0 - learning * decay_rate) - learning * (
        first_next / first_fix
    ) / (jnp.sqrt(second_next / second_fix) + epsilon)
    return stepped.astype(jnp.bfloat16), first_next, second_next


def migrate(state, group_source, groups):
    layers, rows_dev, width = state.shape
    piece_rows = rows_dev // groups
    split = state.reshape(layers, groups, piece_rows, width)
    spread = lax.all_to_all(split, "grp", split_axis=1, concat_axis=1, tiled=True)
    chosen = jnp.take(spread, group_source, axis=1, mode="clip", unique_indices=True)
    home = lax.all_to_all(chosen, "grp", split_axis=1, concat_axis=1, tiled=True)
    return home.reshape(layers, rows_dev, width)


def pack_tokens(token_block, route_block, gate_block, limit, hot_index, capacity):
    valid = jnp.arange(token_block.shape[0], dtype=jnp.int32) < limit
    hits = (route_block[:, :, None] == hot_index[None, None, :]) & valid[:, None, None]
    named = jnp.sum(hits.astype(jnp.int32), axis=1)
    scales = jnp.sum(jnp.where(hits, gate_block.astype(jnp.float32)[:, :, None], 0.0), axis=1)
    ranks = jnp.cumsum(named, axis=0) - named
    slots = jnp.arange(capacity, dtype=jnp.int32)
    placed = (ranks.T[:, None, :] == slots[None, :, None]) & (named.T[:, None, :] == 1)
    packed = jnp.einsum(
        "hct,td->hcd", placed.astype(jnp.bfloat16), token_block, preferred_element_type=jnp.float32
    ).astype(jnp.bfloat16)
    gate_scale = jnp.einsum("hct,th->hc", placed.astype(jnp.float32), scales).astype(jnp.bfloat16)
    return (packed, gate_scale)


def local(
    prev_acts,
    prev_cot,
    weights,
    first_moment,
    second_moment,
    tokens,
    routing,
    gates,
    token_counts,
    old_owner,
    new_owner,
):
    groups = lax.axis_size("grp")
    experts = groups * GRP
    token_slots = tokens.shape[2]
    capacity = min(token_slots, 3 * token_slots // groups)
    width = weights.shape[2]
    hidden_units = width // 2
    activations = prev_acts[0, 0]
    cotangent = prev_cot[0, 0]
    hot_index = jnp.arange(groups, dtype=jnp.int32)
    holder = jnp.sum(
        jnp.where(new_owner[None, :] == hot_index[:, None], hot_index[None, :], 0), axis=1
    )
    group_source = jnp.take(old_owner, holder)

    packed, gate_scale = pack_tokens(
        tokens[0, 0], routing[0, 0], gates[0, 0], token_counts[0, 0], holder, capacity
    )
    scale_cols = jnp.zeros((groups, capacity, SCALE_PAD), jnp.bfloat16).at[:, :, 0].set(gate_scale)
    payload = jnp.concatenate([packed, scale_cols], axis=2)
    half = capacity // 2
    by_first = lax.all_to_all(payload[:, :half], "grp", split_axis=0, concat_axis=0, tiled=True)

    grads = lax.psum_scatter(
        lax.dot_general(
            activations, cotangent, (((0,), (0,)), ((), ())), preferred_element_type=jnp.float32
        ).astype(jnp.bfloat16),
        "dp",
        scatter_dimension=0,
        tiled=True,
    )
    by_first, grads = lax.optimization_barrier((by_first, grads))
    grads = grads.astype(jnp.float32)
    stepped, first_next, second_next = adamw(weights[0], first_moment[0], second_moment[0], grads)
    new_weight = migrate(stepped[None], group_source, groups)[0]
    second, new_weight = lax.optimization_barrier((payload[:, half:], new_weight))
    by_second = lax.all_to_all(second, "grp", split_axis=0, concat_axis=0, tiled=True)
    moments = jnp.stack([first_next.astype(jnp.bfloat16), second_next.astype(jnp.bfloat16)])
    moments, by_second = lax.optimization_barrier((moments, by_second))
    moved = migrate(moments, group_source, groups)
    from_ylo = lax.ppermute(by_second, "ylo", perm=[(0, 1), (1, 0)])
    near = [
        lax.all_gather(by_first, "ylo", axis=0, tiled=False),
        jnp.stack([by_second, from_ylo]),
    ]
    near = [n.reshape(2 * groups * half, D + SCALE_PAD) for n in near]

    both = lax.all_gather(new_weight, ("xhi", "dp"), axis=0, tiled=True)
    both = both.reshape(2, -1, width)
    both = jnp.pad(both, ((0, 0), (0, SCALE_PAD), (0, 0)))
    projected = jnp.stack(
        [
            jnp.stack([jnp.dot(n, both[k], preferred_element_type=jnp.float32) for n in near])
            for k in range(2)
        ]
    )
    scaling = jnp.stack([n[:, D] for n in near]).astype(jnp.float32)
    result = (
        jax.nn.silu(projected[..., :hidden_units])
        * projected[..., hidden_units:]
        * scaling[None, :, :, None]
    ).astype(jnp.bfloat16)
    xhi = lax.axis_index("xhi")
    own = lax.dynamic_index_in_dim(result, xhi, axis=0, keepdims=False)
    other = lax.dynamic_index_in_dim(result, 1 - xhi, axis=0, keepdims=False)
    for_partner = lax.ppermute(other, "xhi", perm=[(0, 1), (1, 0)])
    mine = jnp.stack([own, for_partner]).reshape(2, 2, 2, groups, half, hidden_units)
    flip = jnp.arange(2, dtype=jnp.int32)
    mine = jnp.take(mine, flip ^ xhi, axis=0)
    ylo = lax.axis_index("ylo")
    mine = jnp.stack([mine[:, 0], jnp.take(mine[:, 1], flip ^ ylo, axis=1)], axis=1)
    hidden = jnp.transpose(mine, (3, 2, 0, 1, 4, 5)).reshape(1, 1, experts * capacity, hidden_units)
    return (
        hidden,
        new_weight[None],
        moved[0].astype(jnp.float32)[None],
        moved[1].astype(jnp.float32)[None],
    )


def solution(mesh):
    n_dp = mesh.shape["dp"]
    n_expert = mesh.shape["expert"]
    mesh4 = Mesh(
        mesh.devices.reshape(n_dp, n_expert // GRP, 2, 2), ("dp", "grp", "ylo", "xhi")
    )
    ex = ("grp", "ylo", "xhi")
    in_specs = (
        P("dp", ex, None, None),
        P("dp", ex, None, None),
        P(ex, "dp", None),
        P(ex, "dp", None),
        P(ex, "dp", None),
        P("dp", ex, None, None),
        P("dp", ex, None, None),
        P("dp", ex, None, None),
        P("dp", ex),
        P(),
        P(),
    )
    out_specs = (
        P("dp", ex, None, None),
        P(ex, "dp", None),
        P(ex, "dp", None),
        P(ex, "dp", None),
    )
    return jax.shard_map(local, mesh=mesh4, in_specs=in_specs, out_specs=out_specs, check_vma=False)
```

```python
import jax
import jax.numpy as jnp
from jax import lax
from jax.sharding import Mesh
from jax.sharding import PartitionSpec as P

D = 3584
GRP = 4
SCALE_PAD = 128


beta_first = 0.9
beta_second = 0.95
learning = 0.00022
decay_rate = 0.1
epsilon = 1e-08
first_fix = 1.0 - 0.9**40
second_fix = 1.0 - 0.95**40


def adamw(weight_now, first_now, second_now, gradient):
    first_next = beta_first * first_now + (1.0 - beta_first) * gradient
    second_next = beta_second * second_now + (1.0 - beta_second) * gradient * gradient
    stepped = weight_now.astype(jnp.float32) * (1.0 - learning * decay_rate) - learning * (
        first_next / first_fix
    ) / (jnp.sqrt(second_next / second_fix) + epsilon)
    return stepped.astype(jnp.bfloat16), first_next, second_next


def migrate(state, group_source, groups):
    layers, rows_dev, width = state.shape
    piece_rows = rows_dev // groups
    split = state.reshape(layers, groups, piece_rows, width)
    spread = lax.all_to_all(split, "grp", split_axis=1, concat_axis=1, tiled=True)
    chosen = jnp.take(spread, group_source, axis=1, mode="clip", unique_indices=True)
    home = lax.all_to_all(chosen, "grp", split_axis=1, concat_axis=1, tiled=True)
    return home.reshape(layers, rows_dev, width)


def pack_tokens(token_block, route_block, gate_block, limit, hot_index, capacity):
    valid = jnp.arange(token_block.shape[0], dtype=jnp.int32) < limit
    hits = (route_block[:, :, None] == hot_index[None, None, :]) & valid[:, None, None]
    named = jnp.sum(hits.astype(jnp.int32), axis=1)
    scales = jnp.sum(jnp.where(hits, gate_block.astype(jnp.float32)[:, :, None], 0.0), axis=1)
    ranks = jnp.cumsum(named, axis=0) - named
    slots = jnp.arange(capacity, dtype=jnp.int32)
    placed = (ranks.T[:, None, :] == slots[None, :, None]) & (named.T[:, None, :] == 1)
    packed = jnp.einsum(
        "hct,td->hcd", placed.astype(jnp.bfloat16), token_block, preferred_element_type=jnp.float32
    ).astype(jnp.bfloat16)
    gate_scale = jnp.einsum("hct,th->hc", placed.astype(jnp.float32), scales).astype(jnp.bfloat16)
    return (packed, gate_scale)


def local(
    prev_acts,
    prev_cot,
    weights,
    first_moment,
    second_moment,
    tokens,
    routing,
    gates,
    token_counts,
    old_owner,
    new_owner,
):
    groups = lax.axis_size("grp")
    experts = groups * GRP
    token_slots = tokens.shape[2]
    capacity = min(token_slots, 3 * token_slots // groups)
    width = weights.shape[2]
    hidden_units = width // 2
    activations = prev_acts[0, 0]
    cotangent = prev_cot[0, 0]
    hot_index = jnp.arange(groups, dtype=jnp.int32)
    holder = jnp.sum(
        jnp.where(new_owner[None, :] == hot_index[:, None], hot_index[None, :], 0), axis=1
    )
    group_source = jnp.take(old_owner, holder)

    packed, gate_scale = pack_tokens(
        tokens[0, 0], routing[0, 0], gates[0, 0], token_counts[0, 0], holder, capacity
    )
    scale_cols = jnp.zeros((groups, capacity, SCALE_PAD), jnp.bfloat16).at[:, :, 0].set(gate_scale)
    payload = jnp.concatenate([packed, scale_cols], axis=2)
    by_group = lax.all_to_all(payload, "grp", split_axis=0, concat_axis=0, tiled=True)

    grads = lax.psum_scatter(
        lax.dot_general(
            activations, cotangent, (((0,), (0,)), ((), ())), preferred_element_type=jnp.float32
        ).astype(jnp.bfloat16),
        "dp",
        scatter_dimension=0,
        tiled=True,
    )
    by_group, grads = lax.optimization_barrier((by_group, grads))
    grads = grads.astype(jnp.float32)
    near = lax.all_gather(by_group, "ylo", axis=0, tiled=False)
    near = near.reshape(2 * groups * capacity, D + SCALE_PAD)
    stepped, first_next, second_next = adamw(weights[0], first_moment[0], second_moment[0], grads)
    new_weight = migrate(stepped[None], group_source, groups)[0]
    moments = jnp.stack([first_next.astype(jnp.bfloat16), second_next.astype(jnp.bfloat16)])
    moments, new_weight = lax.optimization_barrier((moments, new_weight))
    moved = migrate(moments, group_source, groups)

    both = lax.all_gather(new_weight, ("xhi", "dp"), axis=0, tiled=True)
    both = both.reshape(2, -1, width)
    both = jnp.pad(both, ((0, 0), (0, SCALE_PAD), (0, 0)))
    scaling = near[:, D].astype(jnp.float32)
    xhi = lax.axis_index("xhi")

    def swiglu(weight_set):
        projected = jnp.dot(near, weight_set, preferred_element_type=jnp.float32)
        result = (
            jax.nn.silu(projected[:, :hidden_units])
            * projected[:, hidden_units:]
            * scaling[:, None]
        )
        return result.astype(jnp.bfloat16)

    other = swiglu(lax.dynamic_index_in_dim(both, 1 - xhi, axis=0, keepdims=False))
    for_partner = lax.ppermute(other, "xhi", perm=[(0, 1), (1, 0)])
    own = swiglu(lax.dynamic_index_in_dim(both, xhi, axis=0, keepdims=False))
    mine = jnp.stack([own, for_partner]).reshape(2, 2, groups, capacity, hidden_units)
    flip = jnp.arange(2, dtype=jnp.int32)
    mine = jnp.take(mine, flip ^ xhi, axis=0)
    hidden = jnp.transpose(mine, (2, 1, 0, 3, 4)).reshape(1, 1, experts * capacity, hidden_units)
    return (
        hidden,
        new_weight[None],
        moved[0].astype(jnp.float32)[None],
        moved[1].astype(jnp.float32)[None],
    )


def solution(mesh):
    n_dp = mesh.shape["dp"]
    n_expert = mesh.shape["expert"]
    mesh4 = Mesh(
        mesh.devices.reshape(n_dp, n_expert // GRP, 2, 2), ("dp", "grp", "ylo", "xhi")
    )
    ex = ("grp", "ylo", "xhi")
    in_specs = (
        P("dp", ex, None, None),
        P("dp", ex, None, None),
        P(ex, "dp", None),
        P(ex, "dp", None),
        P(ex, "dp", None),
        P("dp", ex, None, None),
        P("dp", ex, None, None),
        P("dp", ex, None, None),
        P("dp", ex),
        P(),
        P(),
    )
    out_specs = (
        P("dp", ex, None, None),
        P(ex, "dp", None),
        P(ex, "dp", None),
        P(ex, "dp", None),
    )
    return jax.shard_map(local, mesh=mesh4, in_specs=in_specs, out_specs=out_specs, check_vma=False)
```

```python
import jax
import jax.numpy as jnp
from jax import lax
from jax.sharding import Mesh
from jax.sharding import PartitionSpec as P

D = 3584
GRP = 4
SCALE_PAD = 128


beta_first = 0.9
beta_second = 0.95
learning = 0.00022
decay_rate = 0.1
epsilon = 1e-08
first_fix = 1.0 - 0.9**40
second_fix = 1.0 - 0.95**40


def adamw(weight_now, first_now, second_now, gradient):
    first_next = beta_first * first_now + (1.0 - beta_first) * gradient
    second_next = beta_second * second_now + (1.0 - beta_second) * gradient * gradient
    stepped = weight_now.astype(jnp.float32) * (1.0 - learning * decay_rate) - learning * (
        first_next / first_fix
    ) / (jnp.sqrt(second_next / second_fix) + epsilon)
    return stepped.astype(jnp.bfloat16), first_next, second_next


def migrate(state, group_source, groups, mode=None):
    layers, rows_dev, width = state.shape
    piece_rows = rows_dev // groups
    split = state.reshape(layers, groups, piece_rows, width)
    spread = lax.all_to_all(split, "grp", split_axis=1, concat_axis=1, tiled=True)
    chosen = jnp.take(spread, group_source, axis=1, mode=mode)
    home = lax.all_to_all(chosen, "grp", split_axis=1, concat_axis=1, tiled=True)
    return home.reshape(layers, rows_dev, width)


def pack_tokens(token_block, route_block, gate_block, limit, hot_index, capacity):
    valid = jnp.arange(token_block.shape[0], dtype=jnp.int32) < limit
    hits = (route_block[:, :, None] == hot_index[None, None, :]) & valid[:, None, None]
    named = jnp.sum(hits.astype(jnp.int32), axis=1)
    scales = jnp.sum(jnp.where(hits, gate_block.astype(jnp.float32)[:, :, None], 0.0), axis=1)
    ranks = jnp.cumsum(named, axis=0) - named
    slots = jnp.arange(capacity, dtype=jnp.int32)
    placed = (ranks.T[:, None, :] == slots[None, :, None]) & (named.T[:, None, :] == 1)
    packed = jnp.einsum(
        "hct,td->hcd", placed.astype(jnp.bfloat16), token_block, preferred_element_type=jnp.float32
    ).astype(jnp.bfloat16)
    gate_scale = jnp.einsum("hct,th->hc", placed.astype(jnp.float32), scales).astype(jnp.bfloat16)
    return (packed, gate_scale)


def local(
    prev_acts,
    prev_cot,
    weights,
    first_moment,
    second_moment,
    tokens,
    routing,
    gates,
    token_counts,
    old_owner,
    new_owner,
):
    groups = lax.axis_size("grp")
    experts = groups * GRP
    token_slots = tokens.shape[2]
    capacity = min(token_slots, 3 * token_slots // groups)
    width = weights.shape[2]
    hidden_units = width // 2
    activations = prev_acts[0, 0]
    cotangent = prev_cot[0, 0]
    hot_index = jnp.arange(groups, dtype=jnp.int32)
    holder = jnp.sum(
        jnp.where(new_owner[None, :] == hot_index[:, None], hot_index[None, :], 0), axis=1
    )
    group_source = jnp.take(old_owner, holder)

    packed, gate_scale = pack_tokens(
        tokens[0, 0], routing[0, 0], gates[0, 0], token_counts[0, 0], holder, capacity
    )
    scale_cols = jnp.zeros((groups, capacity, SCALE_PAD), jnp.bfloat16).at[:, :, 0].set(gate_scale)
    payload = jnp.concatenate([packed, scale_cols], axis=2)
    by_group = lax.all_to_all(payload, "grp", split_axis=0, concat_axis=0, tiled=True)

    grads = lax.psum_scatter(
        lax.dot_general(
            activations, cotangent, (((0,), (0,)), ((), ())), preferred_element_type=jnp.float32
        ).astype(jnp.bfloat16),
        "dp",
        scatter_dimension=0,
        tiled=True,
    )
    by_group, grads = lax.optimization_barrier((by_group, grads))
    grads = grads.astype(jnp.float32)
    near = lax.all_gather(by_group, "ylo", axis=0, tiled=False)
    near = near.reshape(2 * groups * capacity, D + SCALE_PAD)
    stepped, first_next, second_next = adamw(weights[0], first_moment[0], second_moment[0], grads)
    weight_home = migrate(stepped[None], group_source, groups)
    new_weight = weight_home[0]
    moments = jnp.stack([first_next.astype(jnp.bfloat16), second_next.astype(jnp.bfloat16)])
    moments, new_weight = lax.optimization_barrier((moments, new_weight))
    moved = migrate(moments, group_source, groups, mode="clip")

    both = lax.all_gather(new_weight, ("xhi", "dp"), axis=0, tiled=True)
    both = both.reshape(2, -1, width)
    both = jnp.pad(both, ((0, 0), (0, SCALE_PAD), (0, 0)))
    projected = jnp.stack(
        [jnp.dot(near, both[k], preferred_element_type=jnp.float32) for k in range(2)]
    )
    scaling = near[:, D].astype(jnp.float32)
    result = (
        jax.nn.silu(projected[:, :, :hidden_units])
        * projected[:, :, hidden_units:]
        * scaling[None, :, None]
    ).astype(jnp.bfloat16)
    xhi = lax.axis_index("xhi")
    own = lax.dynamic_index_in_dim(result, xhi, axis=0, keepdims=False)
    other = lax.dynamic_index_in_dim(result, 1 - xhi, axis=0, keepdims=False)
    for_partner = lax.ppermute(other, "xhi", perm=[(0, 1), (1, 0)])
    mine = jnp.stack([own, for_partner]).reshape(2, 2, groups, capacity, hidden_units)
    flip = jnp.arange(2, dtype=jnp.int32)
    mine = jnp.take(mine, flip ^ xhi, axis=0)
    hidden = jnp.transpose(mine, (2, 1, 0, 3, 4)).reshape(1, 1, experts * capacity, hidden_units)
    return (
        hidden,
        weight_home,
        moved[0].astype(jnp.float32)[None],
        moved[1].astype(jnp.float32)[None],
    )


def solution(mesh):
    n_dp = mesh.shape["dp"]
    n_expert = mesh.shape["expert"]
    mesh4 = Mesh(
        mesh.devices.reshape(n_dp, n_expert // GRP, 2, 2), ("dp", "grp", "ylo", "xhi")
    )
    ex = ("grp", "ylo", "xhi")
    in_specs = (
        P("dp", ex, None, None),
        P("dp", ex, None, None),
        P(ex, "dp", None),
        P(ex, "dp", None),
        P(ex, "dp", None),
        P("dp", ex, None, None),
        P("dp", ex, None, None),
        P("dp", ex, None, None),
        P("dp", ex),
        P(),
        P(),
    )
    out_specs = (
        P("dp", ex, None, None),
        P(ex, "dp", None),
        P(ex, "dp", None),
        P(ex, "dp", None),
    )
    return jax.shard_map(local, mesh=mesh4, in_specs=in_specs, out_specs=out_specs, check_vma=False)
```

```python
import jax
import jax.numpy as jnp
from jax import lax
from jax.sharding import Mesh
from jax.sharding import PartitionSpec as P

D = 3584
GRP = 4
SCALE_PAD = 128


beta_first = 0.9
beta_second = 0.95
learning = 0.00022
decay_rate = 0.1
epsilon = 1e-08
first_fix = 1.0 - 0.9**40
second_fix = 1.0 - 0.95**40


def adamw(weight_now, first_now, second_now, gradient):
    first_next = beta_first * first_now + (1.0 - beta_first) * gradient
    second_next = beta_second * second_now + (1.0 - beta_second) * gradient * gradient
    stepped = weight_now.astype(jnp.float32) * (1.0 - learning * decay_rate) - learning * (
        first_next / first_fix
    ) / (jnp.sqrt(second_next / second_fix) + epsilon)
    return stepped.astype(jnp.bfloat16), first_next, second_next


def migrate(state, group_source, groups, mode=None):
    layers, rows_dev, width = state.shape
    piece_rows = rows_dev // groups
    split = state.reshape(layers, groups, piece_rows, width)
    spread = lax.all_to_all(split, "grp", split_axis=1, concat_axis=1, tiled=True)
    chosen = jnp.take(spread, group_source, axis=1, mode=mode)
    home = lax.all_to_all(chosen, "grp", split_axis=1, concat_axis=1, tiled=True)
    return home.reshape(layers, rows_dev, width)


def pack_tokens(token_block, route_block, gate_block, limit, hot_index, capacity):
    valid = jnp.arange(token_block.shape[0], dtype=jnp.int32) < limit
    hits = (route_block[:, :, None] == hot_index[None, None, :]) & valid[:, None, None]
    named = jnp.sum(hits.astype(jnp.int32), axis=1)
    scales = jnp.sum(jnp.where(hits, gate_block.astype(jnp.float32)[:, :, None], 0.0), axis=1)
    ranks = jnp.cumsum(named, axis=0) - named
    slots = jnp.arange(capacity, dtype=jnp.int32)
    placed = (ranks.T[:, None, :] == slots[None, :, None]) & (named.T[:, None, :] == 1)
    packed = jnp.einsum(
        "hct,td->hcd", placed.astype(jnp.bfloat16), token_block, preferred_element_type=jnp.float32
    ).astype(jnp.bfloat16)
    gate_scale = jnp.einsum("hct,th->hc", placed.astype(jnp.float32), scales).astype(jnp.bfloat16)
    return (packed, gate_scale)


def local(
    prev_acts,
    prev_cot,
    weights,
    first_moment,
    second_moment,
    tokens,
    routing,
    gates,
    token_counts,
    old_owner,
    new_owner,
):
    groups = lax.axis_size("grp")
    experts = groups * GRP
    token_slots = tokens.shape[2]
    capacity = min(token_slots, 3 * token_slots // groups)
    width = weights.shape[2]
    hidden_units = width // 2
    activations = prev_acts[0, 0]
    cotangent = prev_cot[0, 0]
    hot_index = jnp.arange(groups, dtype=jnp.int32)
    holder = jnp.sum(
        jnp.where(new_owner[None, :] == hot_index[:, None], hot_index[None, :], 0), axis=1
    )
    group_source = jnp.take(old_owner, holder)

    packed, gate_scale = pack_tokens(
        tokens[0, 0], routing[0, 0], gates[0, 0], token_counts[0, 0], holder, capacity
    )
    scale_cols = jnp.zeros((groups, capacity, SCALE_PAD), jnp.bfloat16).at[:, :, 0].set(gate_scale)
    payload = jnp.concatenate([packed, scale_cols], axis=2)
    by_group = lax.all_to_all(payload, "grp", split_axis=0, concat_axis=0, tiled=True)

    grads = lax.psum_scatter(
        lax.dot_general(
            activations, cotangent, (((0,), (0,)), ((), ())), preferred_element_type=jnp.float32
        ).astype(jnp.bfloat16),
        "dp",
        scatter_dimension=0,
        tiled=True,
    )
    by_group, grads = lax.optimization_barrier((by_group, grads))
    grads = grads.astype(jnp.float32)
    near = lax.all_gather(by_group, "ylo", axis=0, tiled=False)
    near = near.reshape(2 * groups * capacity, D + SCALE_PAD)
    stepped, first_next, second_next = adamw(weights[0], first_moment[0], second_moment[0], grads)
    weight_home = migrate(stepped[None], group_source, groups)
    new_weight = weight_home[0]
    moments = jnp.stack([first_next.astype(jnp.bfloat16), second_next.astype(jnp.bfloat16)])
    moments, new_weight = lax.optimization_barrier((moments, new_weight))
    moved = migrate(moments, group_source, groups, mode="clip")

    both = lax.all_gather(new_weight, ("xhi", "dp"), axis=0, tiled=True)
    both = both.reshape(2, -1, width)
    both = jnp.pad(both, ((0, 0), (0, SCALE_PAD), (0, 0)))
    projected = jnp.stack(
        [jnp.dot(near, both[k], preferred_element_type=jnp.float32) for k in range(2)]
    )
    scaling = near[:, D].astype(jnp.float32)
    result = (
        jax.nn.silu(projected[:, :, :hidden_units])
        * projected[:, :, hidden_units:]
        * scaling[None, :, None]
    ).astype(jnp.bfloat16)
    xhi = lax.axis_index("xhi")
    own = lax.dynamic_index_in_dim(result, xhi, axis=0, keepdims=False)
    other = lax.dynamic_index_in_dim(result, 1 - xhi, axis=0, keepdims=False)
    for_partner = lax.ppermute(other, "xhi", perm=[(0, 1), (1, 0)])
    mine = jnp.where(
        xhi == 0, jnp.stack([own, for_partner]), jnp.stack([for_partner, own])
    ).reshape(2, 2, groups, capacity, hidden_units)
    hidden = jnp.transpose(mine, (2, 1, 0, 3, 4)).reshape(1, 1, experts * capacity, hidden_units)
    return (
        hidden,
        weight_home,
        moved[0].astype(jnp.float32)[None],
        moved[1].astype(jnp.float32)[None],
    )


def solution(mesh):
    n_dp = mesh.shape["dp"]
    n_expert = mesh.shape["expert"]
    mesh4 = Mesh(
        mesh.devices.reshape(n_dp, n_expert // GRP, 2, 2), ("dp", "grp", "ylo", "xhi")
    )
    ex = ("grp", "ylo", "xhi")
    in_specs = (
        P("dp", ex, None, None),
        P("dp", ex, None, None),
        P(ex, "dp", None),
        P(ex, "dp", None),
        P(ex, "dp", None),
        P("dp", ex, None, None),
        P("dp", ex, None, None),
        P("dp", ex, None, None),
        P("dp", ex),
        P(),
        P(),
    )
    out_specs = (
        P("dp", ex, None, None),
        P(ex, "dp", None),
        P(ex, "dp", None),
        P(ex, "dp", None),
    )
    return jax.shard_map(local, mesh=mesh4, in_specs=in_specs, out_specs=out_specs, check_vma=False)
```

```python
import jax
import jax.numpy as jnp
from jax import lax
from jax.sharding import Mesh
from jax.sharding import PartitionSpec as P

D = 3584
GRP = 4
SCALE_PAD = 128


beta_first = 0.9
beta_second = 0.95
learning = 0.00022
decay_rate = 0.1
epsilon = 1e-08
first_fix = 1.0 - 0.9**40
second_fix = 1.0 - 0.95**40


def adamw(weight_now, first_now, second_now, gradient):
    first_next = beta_first * first_now + (1.0 - beta_first) * gradient
    second_next = beta_second * second_now + (1.0 - beta_second) * gradient * gradient
    stepped = weight_now.astype(jnp.float32) * (1.0 - learning * decay_rate) - learning * (
        first_next / first_fix
    ) / (jnp.sqrt(second_next / second_fix) + epsilon)
    return stepped.astype(jnp.bfloat16), first_next, second_next


def migrate(state, group_source, groups, mode=None):
    layers, rows_dev, width = state.shape
    piece_rows = rows_dev // groups
    split = state.reshape(layers, groups, piece_rows, width)
    spread = lax.all_to_all(split, "grp", split_axis=1, concat_axis=1, tiled=True)
    chosen = jnp.take(spread, group_source, axis=1, mode=mode)
    home = lax.all_to_all(chosen, "grp", split_axis=1, concat_axis=1, tiled=True)
    return home.reshape(layers, rows_dev, width)


def pack_tokens(token_block, route_block, gate_block, limit, hot_index, capacity):
    valid = jnp.arange(token_block.shape[0], dtype=jnp.int32) < limit
    hits = (route_block[:, :, None] == hot_index[None, None, :]) & valid[:, None, None]
    named = jnp.sum(hits.astype(jnp.int32), axis=1)
    scales = jnp.sum(jnp.where(hits, gate_block.astype(jnp.float32)[:, :, None], 0.0), axis=1)
    ranks = jnp.cumsum(named, axis=0) - named
    slots = jnp.arange(capacity, dtype=jnp.int32)
    placed = (ranks.T[:, None, :] == slots[None, :, None]) & (named.T[:, None, :] == 1)
    packed = jnp.einsum(
        "hct,td->hcd", placed.astype(jnp.bfloat16), token_block, preferred_element_type=jnp.float32
    ).astype(jnp.bfloat16)
    gate_scale = jnp.einsum("hct,th->hc", placed.astype(jnp.float32), scales).astype(jnp.bfloat16)
    return (packed, gate_scale)


def local(
    prev_acts,
    prev_cot,
    weights,
    first_moment,
    second_moment,
    tokens,
    routing,
    gates,
    token_counts,
    old_owner,
    new_owner,
):
    groups = lax.axis_size("grp")
    experts = groups * GRP
    token_slots = tokens.shape[2]
    capacity = min(token_slots, 3 * token_slots // groups)
    width = weights.shape[2]
    hidden_units = width // 2
    activations = prev_acts[0, 0]
    cotangent = prev_cot[0, 0]
    hot_index = jnp.arange(groups, dtype=jnp.int32)
    holder = jnp.sum(
        jnp.where(new_owner[None, :] == hot_index[:, None], hot_index[None, :], 0), axis=1
    )
    group_source = jnp.take(old_owner, holder)

    packed, gate_scale = pack_tokens(
        tokens[0, 0], routing[0, 0], gates[0, 0], token_counts[0, 0], holder, capacity
    )
    scale_cols = jnp.zeros((groups, capacity, SCALE_PAD), jnp.bfloat16).at[:, :, 0].set(gate_scale)
    payload = jnp.concatenate([packed, scale_cols], axis=2)
    by_group = lax.all_to_all(payload, "grp", split_axis=0, concat_axis=0, tiled=True)

    grads = lax.psum_scatter(
        lax.dot_general(
            activations, cotangent, (((0,), (0,)), ((), ())), preferred_element_type=jnp.float32
        ).astype(jnp.bfloat16),
        "dp",
        scatter_dimension=0,
        tiled=True,
    )
    by_group, grads = lax.optimization_barrier((by_group, grads))
    grads = grads.astype(jnp.float32)
    near = lax.all_gather(by_group, "ylo", axis=0, tiled=False)
    near = near.reshape(2 * groups * capacity, D + SCALE_PAD)
    stepped, first_next, second_next = adamw(weights[0], first_moment[0], second_moment[0], grads)
    weight_home = migrate(stepped[None], group_source, groups, mode="clip")
    new_weight = weight_home[0]
    moments = jnp.stack([first_next.astype(jnp.bfloat16), second_next.astype(jnp.bfloat16)])
    moments, new_weight = lax.optimization_barrier((moments, new_weight))
    moved = migrate(moments, group_source, groups, mode="clip")

    both = lax.all_gather(new_weight, ("xhi", "dp"), axis=0, tiled=True)
    both = both.reshape(2, -1, width)
    both = jnp.pad(both, ((0, 0), (0, SCALE_PAD), (0, 0)))
    projected = jnp.stack(
        [jnp.dot(near, both[k], preferred_element_type=jnp.float32) for k in range(2)]
    )
    scaling = near[:, D].astype(jnp.float32)
    result = (
        jax.nn.silu(projected[:, :, :hidden_units])
        * projected[:, :, hidden_units:]
        * scaling[None, :, None]
    ).astype(jnp.bfloat16)
    xhi = lax.axis_index("xhi")
    own = lax.dynamic_index_in_dim(result, xhi, axis=0, keepdims=False)
    other = lax.dynamic_index_in_dim(result, 1 - xhi, axis=0, keepdims=False)
    for_partner = lax.ppermute(other, "xhi", perm=[(0, 1), (1, 0)])
    mine = jnp.stack([own, for_partner]).reshape(2, 2, groups, capacity, hidden_units)
    flip = jnp.arange(2, dtype=jnp.int32)
    mine = jnp.take(mine, flip ^ xhi, axis=0)
    hidden = jnp.transpose(mine, (2, 1, 0, 3, 4)).reshape(1, 1, experts * capacity, hidden_units)
    return (
        hidden,
        weight_home,
        moved[0].astype(jnp.float32)[None],
        moved[1].astype(jnp.float32)[None],
    )


def solution(mesh):
    n_dp = mesh.shape["dp"]
    n_expert = mesh.shape["expert"]
    mesh4 = Mesh(
        mesh.devices.reshape(n_dp, n_expert // GRP, 2, 2), ("dp", "grp", "ylo", "xhi")
    )
    ex = ("grp", "ylo", "xhi")
    in_specs = (
        P("dp", ex, None, None),
        P("dp", ex, None, None),
        P(ex, "dp", None),
        P(ex, "dp", None),
        P(ex, "dp", None),
        P("dp", ex, None, None),
        P("dp", ex, None, None),
        P("dp", ex, None, None),
        P("dp", ex),
        P(),
        P(),
    )
    out_specs = (
        P("dp", ex, None, None),
        P(ex, "dp", None),
        P(ex, "dp", None),
        P(ex, "dp", None),
    )
    return jax.shard_map(local, mesh=mesh4, in_specs=in_specs, out_specs=out_specs, check_vma=False)
```
